32 devices in a mesh: sub: 8 (over z, x), coarse: 4 (over y, core).
Axes of the slice: x: 2, y: 2, z: 4, core: 2. Of those that a mesh axis runs over, the one named last changes fastest.
Arguments:
- residual: bfloat16 [128, 512, 256], P(('sub', 'coarse')), may hold values from -6 to 6
- margin: int32 [128, 4], P(('sub', 'coarse')), may hold values from 0 to 5, as said below
- inverse_blocks: bfloat16 [128, 4, 256, 256], P(('sub', 'coarse')), may hold values from -0.1875 to 0.1875
- interface: int32 [128, 2], P(('sub', 'coarse')), may hold values from 0 to 11, as said below
- basis: bfloat16 [128, 2, 256, 128], P(('sub', 'coarse')), may hold values from -0.375 to 0.375
- coarse_pattern: int32 [12, 4], P('coarse'), may hold values from 0 to 11, as said below
- coarse_inverse: bfloat16 [12, 4, 128, 128], P('coarse'), may hold values from -0.0546875 to 0.0546875
Outputs:
- correction: bfloat16 [128, 512, 256], P(('sub', 'coarse'))
The draws below stay inside these ranges and needn't reach their ends.
Inputs may be any that keep to these rules, and one draw needn't show every extreme that they name: margin[j, 0] is j's own slot j % 4 + 1; the first block of each subdomain has slot 0 in entry 1 and the last has slot 5 in entry 2. interface[j, 0] = j % 12. coarse_pattern[n, 0] = n.
All inputs are finite; a program needn't handle non-finite values.
Results may differ from the reference program's by a relative error of at most 0.0051.
Values may be sent and summed in bfloat16 or wider, within the bound.
No kernel may reach another device: no remote copies, remote signals or barrier semaphores. Data moves between devices by JAX's collectives and lax.ppermute only.
A program may use at most 64 MiB of HBM per device.

```python
import jax
import jax.numpy as jnp
from jax import lax

B = 256
CB = 128
BLK_DEV = 4
RHS = 512
OVL = 4
NIF = 2
PC = 4
NB = 128
NCB = 12


def draw_margin(key, part):
    rows = jnp.arange(NB, dtype=jnp.int32)
    within = rows % BLK_DEV
    others = jax.random.randint(key, (NB, OVL - 1), 0, BLK_DEV + 2).astype(jnp.int32)
    first = jnp.where(within == 0, 0, others[:, 0])
    second = jnp.where(within == BLK_DEV - 1, BLK_DEV + 1, others[:, 1])
    return jnp.concatenate([(within + 1)[:, None], first[:, None], second[:, None], others[:, 2:]], axis=1).astype(jnp.int32)


def draw_interface(key, part):
    rows = jnp.arange(NB, dtype=jnp.int32)
    first = rows % NCB
    second = jax.random.randint(key, (NB,), 0, NCB).astype(jnp.int32)
    return jnp.stack([first, second], axis=1).astype(jnp.int32)


def draw_coarse_pattern(key, part):
    rows = jnp.arange(NCB, dtype=jnp.int32)
    others = jax.random.randint(key, (NCB, PC - 1), 0, NCB).astype(jnp.int32)
    return jnp.concatenate([rows[:, None], others], axis=1).astype(jnp.int32)


def levels(rng, shape, cuts, least, top_value):
    level = 1.0
    for dim, shards_of in cuts:
        draws = jax.random.uniform(jax.random.fold_in(jax.random.fold_in(rng, 6), dim), (shards_of,), jnp.float32, least / len(cuts), top_value / len(cuts))
        level = level * jnp.repeat(jnp.exp(draws), shape[dim] // shards_of).reshape((-1,) + (1,) * (len(shape) - 1 - dim))
    return level


def normal_values(key, dims, width, bound, split=(), kind=jnp.bfloat16):
    gain = levels(key, dims, split, -0.22, 0.18) if split else 1.0
    array = jax.random.normal(key, dims, jnp.float32) * width * gain
    return jnp.minimum(jnp.maximum(array, -bound), bound).astype(kind)


def setup_inputs(seed: int = 0) -> dict:
    arg_keys = jax.random.split(jax.random.key(seed), 8)
    return {
        "residual": normal_values(arg_keys[0], (NB, RHS, B), 1.0, 6.0, ((0, 32),)),
        "margin": draw_margin(jax.random.fold_in(arg_keys[7], 71), 0),
        "inverse_blocks": normal_values(arg_keys[2], (NB, OVL, B, B), (OVL * B) ** -0.5, 0.1875, ((0, 32),)),
        "interface": draw_interface(jax.random.fold_in(arg_keys[7], 71), 0),
        "basis": normal_values(arg_keys[4], (NB, NIF, B, CB), (NIF * CB) ** -0.5, 0.375, ((0, 32),)),
        "coarse_pattern": draw_coarse_pattern(jax.random.fold_in(arg_keys[7], 71), 0),
        "coarse_inverse": normal_values(arg_keys[6], (NCB, PC, CB, CB), (PC * B * NB // NCB) ** -0.5, 0.0546875, ((0, 4),)),
    }


def reference(residual, margin, inverse_blocks, interface, basis, coarse_pattern, coarse_inverse):
    count = residual.shape[0] // BLK_DEV
    blocks = residual.reshape(count, BLK_DEV, RHS, B)
    empty = jnp.zeros((1, 1, RHS, B), jnp.bfloat16)
    left = jnp.concatenate([empty, blocks[:-1, -1:]], axis=0)
    right = jnp.concatenate([blocks[1:, :1], empty], axis=0)
    extended = jnp.concatenate([left, blocks, right], axis=1)
    slots = margin.reshape(count, BLK_DEV, OVL)
    factors = inverse_blocks.reshape(count, BLK_DEV, OVL, B, B)
    links = interface.reshape(count, BLK_DEV, NIF)
    values = basis.reshape(count, BLK_DEV, NIF, B, CB)

    def restrict(total, items):
        own, link, value = items
        terms = jnp.einsum("jrb,jqbc->jqrc", own.astype(jnp.float32), value.astype(jnp.float32))
        return total.at[link.reshape(-1)].add(terms.reshape(-1, RHS, CB)), None

    restricted, unused = lax.scan(restrict, jnp.zeros((NCB, RHS, CB), jnp.float32), (blocks, links, values))
    coarse_in = restricted.astype(jnp.bfloat16)
    chosen = coarse_in[coarse_pattern]
    coarse_out = jnp.einsum("nerc,necd->nrd", chosen.astype(jnp.float32), coarse_inverse.astype(jnp.float32)).astype(jnp.bfloat16)

    def finish(items):
        ext, slot, factor, link, value = items
        picked = ext[slot]
        local = jnp.einsum("jerb,jebc->jrc", picked.astype(jnp.float32), factor.astype(jnp.float32))
        lifted = coarse_out[link]
        spread = jnp.einsum("jqrc,jqbc->jrb", lifted.astype(jnp.float32), value.astype(jnp.float32))
        return (local + spread).astype(jnp.bfloat16)

    result = lax.map(finish, (extended, slots, factors, links, values))
    return result.reshape(NB, RHS, B)
```

```python
import jax
import jax.numpy as jnp
from jax import lax
from jax.sharding import PartitionSpec as P


def with_halo(cells, sides, width):
    for axis, dim in sides:
        count = lax.axis_size(axis)
        ends = count - 1
        head = lax.slice_in_dim(cells, 0, width, axis=dim)
        tail = lax.slice_in_dim(cells, cells.shape[dim] - width, cells.shape[dim], axis=dim)
        cells = jnp.concatenate(
            [
                lax.ppermute(tail, axis, [(i, (i + 1) % count) for i in range(ends)]),
                cells,
                lax.ppermute(head, axis, [((i + 1) % count, i) for i in range(ends)]),
            ],
            axis=dim,
        )
    return cells


def coarse_rows(inputs, coarse_pattern, coarse_inverse):
    chosen = jnp.take(inputs, coarse_pattern, axis=0)
    return jnp.einsum(
        "nerc,necd->nrd", chosen, coarse_inverse, preferred_element_type=jnp.float32
    ).astype(jnp.bfloat16)


def per_device(residual, margin, inverse_blocks, interface, basis, coarse_pattern, coarse_inverse):
    pattern_all = lax.all_gather(coarse_pattern, "coarse", axis=0, tiled=True)
    inverse_all = lax.all_gather(coarse_inverse, "coarse", axis=0, tiled=True)
    extended = with_halo(residual, ((("sub", "coarse"), 0),), 1)
    terms = jnp.einsum("jrb,jqbc->jqrc", residual, basis, preferred_element_type=jnp.float32)
    total_blocks = pattern_all.shape[0]
    labels = jnp.arange(total_blocks, dtype=jnp.int32)
    onehot = (interface[:, :, None] == labels[None, None, :]).astype(jnp.float32)
    restricted = jnp.einsum("jqn,jqrc->nrc", onehot, terms, precision=lax.Precision.HIGHEST)
    picked = jnp.take(extended, margin, axis=0)
    local = jnp.einsum("jerb,jebc->jrc", picked, inverse_blocks, preferred_element_type=jnp.float32)
    pattern_all, inverse_all, restricted = lax.optimization_barrier((pattern_all, inverse_all, restricted))
    flat = restricted.reshape(-1, restricted.shape[-1])
    share = lax.psum_scatter(flat, ("sub", "coarse"), scatter_dimension=0, tiled=True)
    coarse_in = lax.all_gather(share.astype(jnp.bfloat16), ("sub", "coarse"), axis=0, tiled=True)
    coarse_out = coarse_rows(coarse_in.reshape(restricted.shape), pattern_all, inverse_all)
    lifted = jnp.take(coarse_out, interface, axis=0)
    spread = jnp.einsum("jqrc,jqbc->jrb", lifted, basis, preferred_element_type=jnp.float32)
    return (local + spread).astype(jnp.bfloat16)


def solution(mesh):
    in_specs = (
        P(("sub", "coarse"), None, None),
        P(("sub", "coarse"), None),
        P(("sub", "coarse"), None, None, None),
        P(("sub", "coarse"), None),
        P(("sub", "coarse"), None, None, None),
        P("coarse", None),
        P("coarse", None, None, None),
    )
    out_specs = P(("sub", "coarse"), None, None)
    return jax.shard_map(
        per_device, mesh=mesh, in_specs=in_specs, out_specs=out_specs, check_vma=False
    )
```

```python
import jax
import jax.numpy as jnp
from jax import lax
from jax.sharding import PartitionSpec as P


def with_halo(cells, sides, width):
    for axis, dim in sides:
        count = lax.axis_size(axis)
        ends = count - 1
        head = lax.slice_in_dim(cells, 0, width, axis=dim)
        tail = lax.slice_in_dim(cells, cells.shape[dim] - width, cells.shape[dim], axis=dim)
        cells = jnp.concatenate(
            [
                lax.ppermute(tail, axis, [(i, (i + 1) % count) for i in range(ends)]),
                cells,
                lax.ppermute(head, axis, [((i + 1) % count, i) for i in range(ends)]),
            ],
            axis=dim,
        )
    return cells


def device_bits():
    bits = []
    for axis in ("coarse", "sub"):
        size = lax.axis_size(axis)
        mask = 1
        while mask < size:
            bits.append((axis, mask))
            mask *= 2
        assert mask == size
    return bits


def bit_of(axis, mask):
    return (lax.axis_index(axis) // mask) % 2


def pairs(axis, mask):
    return [(i, i ^ mask) for i in range(lax.axis_size(axis))]


def halve(x, dim, axis, mask):
    v = bit_of(axis, mask)
    keep = lax.dynamic_index_in_dim(x, v, axis=dim, keepdims=True)
    send = lax.dynamic_index_in_dim(x, 1 - v, axis=dim, keepdims=True)
    return keep + lax.ppermute(send, axis, pairs(axis, mask))


def double(y, dim, axis, mask):
    v = bit_of(axis, mask)
    recv = lax.ppermute(y, axis, pairs(axis, mask))
    return jnp.where(v == 0, jnp.concatenate([y, recv], axis=dim), jnp.concatenate([recv, y], axis=dim))


def stream_orders(nbits, streams):
    rest = list(range(1, nbits))
    orders = []
    for s in range(streams):
        k = (s * len(rest)) // streams
        orders.append([0] + rest[k:] + rest[:k])
    return orders


def per_device(residual, margin, inverse_blocks, interface, basis, coarse_pattern, coarse_inverse):
    pattern_all = lax.all_gather(coarse_pattern, "coarse", axis=0, tiled=True)
    inverse_all = lax.all_gather(coarse_inverse, "coarse", axis=0, tiled=True)
    extended = with_halo(residual, ((("sub", "coarse"), 0),), 1)
    rhs = residual.shape[1]
    width = basis.shape[-1]
    total_blocks = pattern_all.shape[0]
    terms = jnp.einsum("jrb,jqbc->jqrc", residual, basis, preferred_element_type=jnp.float32)
    labels = jnp.arange(total_blocks, dtype=jnp.int32)
    onehot = (interface[:, :, None] == labels[None, None, :]).astype(jnp.float32)
    restricted = jnp.einsum("jqn,jqrc->rnc", onehot, terms, precision=lax.Precision.HIGHEST)

    bits = device_bits()
    nb = len(bits)
    inner = rhs >> nb
    assert inner << nb == rhs
    streams = 3 if total_blocks % 3 == 0 else 1
    per = total_blocks // streams
    orders = stream_orders(nb, streams)
    split = restricted.reshape((2,) * nb + (inner, total_blocks, width))
    parts = [lax.slice_in_dim(split, s * per, (s + 1) * per, axis=nb + 1) for s in range(streams)]
    for step in range(nb):
        parts = [halve(x, orders[s][step], *bits[orders[s][step]]) for s, x in enumerate(parts)]
    mine = jnp.concatenate(parts, axis=nb + 1).reshape(inner, total_blocks, width)
    coarse_in = mine.astype(jnp.bfloat16)
    chosen = jnp.take(coarse_in, pattern_all, axis=1)
    solved = jnp.einsum(
        "rnec,necd->rnd", chosen, inverse_all, preferred_element_type=jnp.float32
    ).astype(jnp.bfloat16)
    solved = solved.reshape((1,) * nb + (inner, total_blocks, width))
    outs = [lax.slice_in_dim(solved, s * per, (s + 1) * per, axis=nb + 1) for s in range(streams)]
    for step in reversed(range(nb)):
        outs = [double(y, orders[s][step], *bits[orders[s][step]]) for s, y in enumerate(outs)]
    coarse_out = jnp.concatenate(outs, axis=nb + 1).reshape(rhs, total_blocks, width)

    picked = jnp.take(extended, margin, axis=0)
    local = jnp.einsum("jerb,jebc->jrc", picked, inverse_blocks, preferred_element_type=jnp.float32)
    lifted = jnp.take(coarse_out, interface, axis=1)
    spread = jnp.einsum("rjqc,jqbc->jrb", lifted, basis, preferred_element_type=jnp.float32)
    return (local + spread).astype(jnp.bfloat16)


def solution(mesh):
    in_specs = (
        P(("sub", "coarse"), None, None),
        P(("sub", "coarse"), None),
        P(("sub", "coarse"), None, None, None),
        P(("sub", "coarse"), None),
        P(("sub", "coarse"), None, None, None),
        P("coarse", None),
        P("coarse", None, None, None),
    )
    out_specs = P(("sub", "coarse"), None, None)
    return jax.shard_map(
        per_device, mesh=mesh, in_specs=in_specs, out_specs=out_specs, check_vma=False
    )
```

```python
import jax
import jax.numpy as jnp
from jax import lax
from jax.sharding import PartitionSpec as P


def with_halo(cells, sides, width):
    for axis, dim in sides:
        count = lax.axis_size(axis)
        ends = count - 1
        head = lax.slice_in_dim(cells, 0, width, axis=dim)
        tail = lax.slice_in_dim(cells, cells.shape[dim] - width, cells.shape[dim], axis=dim)
        cells = jnp.concatenate(
            [
                lax.ppermute(tail, axis, [(i, (i + 1) % count) for i in range(ends)]),
                cells,
                lax.ppermute(head, axis, [((i + 1) % count, i) for i in range(ends)]),
            ],
            axis=dim,
        )
    return cells


def device_bits():
    bits = []
    for axis in ("coarse", "sub"):
        size = lax.axis_size(axis)
        mask = 1
        while mask < size:
            bits.append((axis, mask))
            mask *= 2
        assert mask == size
    return bits


def bit_of(axis, mask):
    return (lax.axis_index(axis) // mask) % 2


def pairs(axis, mask):
    return [(i, i ^ mask) for i in range(lax.axis_size(axis))]


def halve(x, dim, axis, mask):
    v = bit_of(axis, mask)
    keep = lax.dynamic_index_in_dim(x, v, axis=dim, keepdims=True)
    send = lax.dynamic_index_in_dim(x, 1 - v, axis=dim, keepdims=True)
    return keep + lax.ppermute(send, axis, pairs(axis, mask))


def double(y, dim, axis, mask):
    v = bit_of(axis, mask)
    recv = lax.ppermute(y, axis, pairs(axis, mask))
    return jnp.where(v == 0, jnp.concatenate([y, recv], axis=dim), jnp.concatenate([recv, y], axis=dim))


def stream_orders(nbits, streams):
    rest = list(range(1, nbits))
    orders = []
    for s in range(streams):
        k = (s * len(rest)) // streams
        orders.append([0] + rest[k:] + rest[:k])
    return orders


def per_device(residual, margin, inverse_blocks, interface, basis, coarse_pattern, coarse_inverse):
    rows, cols = coarse_inverse.shape[-2:]
    tags = jnp.broadcast_to(coarse_pattern.astype(jnp.bfloat16)[:, :, None, None], coarse_pattern.shape + (8, cols))
    packed = lax.all_gather(jnp.concatenate([coarse_inverse, tags], axis=2), "coarse", axis=0, tiled=True)
    inverse_all = packed[:, :, :rows, :]
    pattern_all = packed[:, :, rows, 0].astype(jnp.int32)
    extended = with_halo(residual, ((("sub", "coarse"), 0),), 1)
    rhs = residual.shape[1]
    width = basis.shape[-1]
    total_blocks = pattern_all.shape[0]
    terms = jnp.einsum("jrb,jqbc->jqrc", residual, basis, preferred_element_type=jnp.float32)
    labels = jnp.arange(total_blocks, dtype=jnp.int32)
    onehot = (interface[:, :, None] == labels[None, None, :]).astype(jnp.float32)
    restricted = jnp.einsum("jqn,jqrc->rnc", onehot, terms, precision=lax.Precision.HIGHEST)

    bits = device_bits()
    nb = len(bits)
    inner = rhs >> nb
    assert inner << nb == rhs
    streams = 3 if total_blocks % 3 == 0 else 1
    per = total_blocks // streams
    orders = stream_orders(nb, streams)
    split = restricted.reshape((2,) * nb + (inner, total_blocks, width))
    parts = [lax.slice_in_dim(split, s * per, (s + 1) * per, axis=nb + 1) for s in range(streams)]
    picked = jnp.take(extended, margin, axis=0)
    local = jnp.einsum("jerb,jebc->jrc", picked, inverse_blocks, preferred_element_type=jnp.float32)
    for step in range(nb):
        parts = [halve(x, orders[s][step], *bits[orders[s][step]]) for s, x in enumerate(parts)]
        if step == 0:
            local, parts = lax.optimization_barrier((local, parts))
    mine = jnp.concatenate(parts, axis=nb + 1).reshape(inner, total_blocks, width)
    coarse_in = mine.astype(jnp.bfloat16)
    chosen = jnp.take(coarse_in, pattern_all, axis=1)
    solved = jnp.einsum(
        "rnec,necd->rnd", chosen, inverse_all, preferred_element_type=jnp.float32
    ).astype(jnp.bfloat16)
    solved = solved.reshape((1,) * nb + (inner, total_blocks, width))
    outs = [lax.slice_in_dim(solved, s * per, (s + 1) * per, axis=nb + 1) for s in range(streams)]
    for step in reversed(range(nb)):
        outs = [double(y, orders[s][step], *bits[orders[s][step]]) for s, y in enumerate(outs)]
    coarse_out = jnp.concatenate(outs, axis=nb + 1).reshape(rhs, total_blocks, width)

    lifted = jnp.take(coarse_out, interface, axis=1)
    spread = jnp.einsum("rjqc,jqbc->jrb", lifted, basis, preferred_element_type=jnp.float32)
    return (local + spread).astype(jnp.bfloat16)


def solution(mesh):
    in_specs = (
        P(("sub", "coarse"), None, None),
        P(("sub", "coarse"), None),
        P(("sub", "coarse"), None, None, None),
        P(("sub", "coarse"), None),
        P(("sub", "coarse"), None, None, None),
        P("coarse", None),
        P("coarse", None, None, None),
    )
    out_specs = P(("sub", "coarse"), None, None)
    return jax.shard_map(
        per_device, mesh=mesh, in_specs=in_specs, out_specs=out_specs, check_vma=False
    )
```

```python
import jax
import jax.numpy as jnp
from jax import lax
from jax.sharding import PartitionSpec as P


def with_halo(cells, sides, width):
    for axis, dim in sides:
        count = lax.axis_size(axis)
        ends = count - 1
        head = lax.slice_in_dim(cells, 0, width, axis=dim)
        tail = lax.slice_in_dim(cells, cells.shape[dim] - width, cells.shape[dim], axis=dim)
        cells = jnp.concatenate(
            [
                lax.ppermute(tail, axis, [(i, (i + 1) % count) for i in range(ends)]),
                cells,
                lax.ppermute(head, axis, [((i + 1) % count, i) for i in range(ends)]),
            ],
            axis=dim,
        )
    return cells


def device_bits():
    bits = []
    for axis in ("coarse", "sub"):
        size = lax.axis_size(axis)
        mask = 1
        while mask < size:
            bits.append((axis, mask))
            mask *= 2
        assert mask == size
    return bits


def bit_of(axis, mask):
    return (lax.axis_index(axis) // mask) % 2


def pairs(axis, mask):
    return [(i, i ^ mask) for i in range(lax.axis_size(axis))]


def halve(x, dim, axis, mask):
    v = bit_of(axis, mask)
    keep = lax.dynamic_index_in_dim(x, v, axis=dim, keepdims=True)
    send = lax.dynamic_index_in_dim(x, 1 - v, axis=dim, keepdims=True)
    return keep + lax.ppermute(send, axis, pairs(axis, mask))


def double(y, dim, axis, mask):
    v = bit_of(axis, mask)
    recv = lax.ppermute(y, axis, pairs(axis, mask))
    return jnp.where(v == 0, jnp.concatenate([y, recv], axis=dim), jnp.concatenate([recv, y], axis=dim))


def stream_orders(nbits, streams):
    rest = list(range(1, nbits))
    orders = []
    for s in range(streams):
        k = (s * len(rest)) // streams
        orders.append([0] + rest[k:] + rest[:k])
    return orders


def per_device(residual, margin, inverse_blocks, interface, basis, coarse_pattern, coarse_inverse):
    rows, cols = coarse_inverse.shape[-2:]
    tags = jnp.broadcast_to(coarse_pattern.astype(jnp.bfloat16)[:, :, None, None], coarse_pattern.shape + (8, cols))
    packed = lax.all_gather(jnp.concatenate([coarse_inverse, tags], axis=2), "coarse", axis=0, tiled=True)
    inverse_all = packed[:, :, :rows, :]
    pattern_all = packed[:, :, rows, 0].astype(jnp.int32)
    extended = with_halo(residual, ((("sub", "coarse"), 0),), 1)
    rhs = residual.shape[1]
    width = basis.shape[-1]
    total_blocks = pattern_all.shape[0]
    terms = jnp.einsum("jrb,jqbc->jqrc", residual, basis, preferred_element_type=jnp.float32)
    labels = jnp.arange(total_blocks, dtype=jnp.int32)
    onehot = (interface[:, :, None] == labels[None, None, :]).astype(jnp.float32)
    restricted = jnp.einsum("jqn,jqrc->rnc", onehot, terms, precision=lax.Precision.HIGHEST)

    bits = device_bits()
    nb = len(bits)
    inner = rhs >> nb
    assert inner << nb == rhs
    streams = 2 if total_blocks % 2 == 0 else 1
    per = total_blocks // streams
    orders = stream_orders(nb, streams)
    split = restricted.reshape((2,) * nb + (inner, total_blocks, width))
    parts = [lax.slice_in_dim(split, s * per, (s + 1) * per, axis=nb + 1) for s in range(streams)]
    picked = jnp.take(extended, margin, axis=0)
    local = jnp.einsum("jerb,jebc->jrc", picked, inverse_blocks, preferred_element_type=jnp.float32)
    for step in range(nb):
        parts = [halve(x, orders[s][step], *bits[orders[s][step]]) for s, x in enumerate(parts)]
        if step == 0:
            local, parts = lax.optimization_barrier((local, parts))
    mine = jnp.concatenate(parts, axis=nb + 1).reshape(inner, total_blocks, width)
    coarse_in = mine.astype(jnp.bfloat16)
    chosen = jnp.take(coarse_in, pattern_all, axis=1)
    solved = jnp.einsum(
        "rnec,necd->rnd", chosen, inverse_all, preferred_element_type=jnp.float32
    ).astype(jnp.bfloat16)
    solved = solved.reshape((1,) * nb + (inner, total_blocks, width))
    outs = [lax.slice_in_dim(solved, s * per, (s + 1) * per, axis=nb + 1) for s in range(streams)]
    for step in reversed(range(nb)):
        outs = [double(y, orders[s][step], *bits[orders[s][step]]) for s, y in enumerate(outs)]
    coarse_out = jnp.concatenate(outs, axis=nb + 1).reshape(rhs, total_blocks, width)

    lifted = jnp.take(coarse_out, interface, axis=1)
    spread = jnp.einsum("rjqc,jqbc->jrb", lifted, basis, preferred_element_type=jnp.float32)
    return (local + spread).astype(jnp.bfloat16)


def solution(mesh):
    in_specs = (
        P(("sub", "coarse"), None, None),
        P(("sub", "coarse"), None),
        P(("sub", "coarse"), None, None, None),
        P(("sub", "coarse"), None),
        P(("sub", "coarse"), None, None, None),
        P("coarse", None),
        P("coarse", None, None, None),
    )
    out_specs = P(("sub", "coarse"), None, None)
    return jax.shard_map(
        per_device, mesh=mesh, in_specs=in_specs, out_specs=out_specs, check_vma=False
    )
```

```python
import jax
import jax.numpy as jnp
from jax import lax
from jax.sharding import PartitionSpec as P


def with_halo(cells, sides, width):
    for axis, dim in sides:
        count = lax.axis_size(axis)
        ends = count - 1
        head = lax.slice_in_dim(cells, 0, width, axis=dim)
        tail = lax.slice_in_dim(cells, cells.shape[dim] - width, cells.shape[dim], axis=dim)
        cells = jnp.concatenate(
            [
                lax.ppermute(tail, axis, [(i, (i + 1) % count) for i in range(ends)]),
                cells,
                lax.ppermute(head, axis, [((i + 1) % count, i) for i in range(ends)]),
            ],
            axis=dim,
        )
    return cells


def device_bits():
    bits = []
    for axis in ("coarse", "sub"):
        size = lax.axis_size(axis)
        mask = 1
        while mask < size:
            bits.append((axis, mask))
            mask *= 2
        assert mask == size
    return bits


def bit_of(axis, mask):
    return (lax.axis_index(axis) // mask) % 2


def pairs(axis, mask):
    return [(i, i ^ mask) for i in range(lax.axis_size(axis))]


def halve(x, dim, axis, mask, wire):
    v = bit_of(axis, mask)
    keep = lax.dynamic_index_in_dim(x, v, axis=dim, keepdims=True)
    send = lax.dynamic_index_in_dim(x, 1 - v, axis=dim, keepdims=True)
    return keep + lax.ppermute(send.astype(wire), axis, pairs(axis, mask)).astype(x.dtype)


def double(y, dim, axis, mask):
    v = bit_of(axis, mask)
    recv = lax.ppermute(y, axis, pairs(axis, mask))
    return jnp.where(v == 0, jnp.concatenate([y, recv], axis=dim), jnp.concatenate([recv, y], axis=dim))


def stream_orders(nbits, streams):
    rest = list(range(1, nbits))
    orders = []
    for s in range(streams):
        k = (s * len(rest)) // streams
        orders.append([0] + rest[k:] + rest[:k])
    return orders


def per_device(residual, margin, inverse_blocks, interface, basis, coarse_pattern, coarse_inverse):
    rows, cols = coarse_inverse.shape[-2:]
    tags = jnp.broadcast_to(coarse_pattern.astype(jnp.bfloat16)[:, :, None, None], coarse_pattern.shape + (8, cols))
    packed = lax.all_gather(jnp.concatenate([coarse_inverse, tags], axis=2), "coarse", axis=0, tiled=True)
    inverse_all = packed[:, :, :rows, :]
    pattern_all = packed[:, :, rows, 0].astype(jnp.int32)
    extended = with_halo(residual, ((("sub", "coarse"), 0),), 1)
    rhs = residual.shape[1]
    width = basis.shape[-1]
    total_blocks = pattern_all.shape[0]
    terms = jnp.einsum("jrb,jqbc->jqrc", residual, basis, preferred_element_type=jnp.float32)
    labels = jnp.arange(total_blocks, dtype=jnp.int32)
    onehot = (interface[:, :, None] == labels[None, None, :]).astype(jnp.float32)
    restricted = jnp.einsum("jqn,jqrc->nrc", onehot, terms, precision=lax.Precision.HIGHEST)

    bits = device_bits()
    nb = len(bits)
    inner = rhs >> nb
    assert inner << nb == rhs
    streams = 3 if total_blocks % 3 == 0 else 1
    per = total_blocks // streams
    orders = stream_orders(nb, streams)
    split = restricted.reshape((total_blocks,) + (2,) * nb + (inner, width))
    parts = [lax.slice_in_dim(split, s * per, (s + 1) * per, axis=0) for s in range(streams)]
    picked = jnp.take(extended, margin, axis=0)
    local = jnp.einsum("jerb,jebc->jrc", picked, inverse_blocks, preferred_element_type=jnp.float32)
    for step in range(nb):
        wire = jnp.float32 if step == 0 else jnp.bfloat16
        parts = [halve(x, 1 + orders[s][step], *bits[orders[s][step]], wire) for s, x in enumerate(parts)]
        if step == 0:
            local, parts = lax.optimization_barrier((local, parts))
    mine = jnp.concatenate(parts, axis=0).reshape(total_blocks, inner, width)
    coarse_in = mine.astype(jnp.bfloat16)
    chosen = jnp.take(coarse_in, pattern_all, axis=0)
    solved = jnp.einsum(
        "nerc,necd->nrd", chosen, inverse_all, preferred_element_type=jnp.float32
    ).astype(jnp.bfloat16)
    solved = solved.reshape((total_blocks,) + (1,) * nb + (inner, width))
    outs = [lax.slice_in_dim(solved, s * per, (s + 1) * per, axis=0) for s in range(streams)]
    for step in reversed(range(nb)):
        outs = [double(y, 1 + orders[s][step], *bits[orders[s][step]]) for s, y in enumerate(outs)]
    coarse_out = jnp.concatenate(outs, axis=0).reshape(total_blocks, rhs, width)

    lifted = jnp.take(coarse_out, interface, axis=0)
    spread = jnp.einsum("jqrc,jqbc->jrb", lifted, basis, preferred_element_type=jnp.float32)
    return (local + spread).astype(jnp.bfloat16)


def solution(mesh):
    in_specs = (
        P(("sub", "coarse"), None, None),
        P(("sub", "coarse"), None),
        P(("sub", "coarse"), None, None, None),
        P(("sub", "coarse"), None),
        P(("sub", "coarse"), None, None, None),
        P("coarse", None),
        P("coarse", None, None, None),
    )
    out_specs = P(("sub", "coarse"), None, None)
    return jax.shard_map(
        per_device, mesh=mesh, in_specs=in_specs, out_specs=out_specs, check_vma=False
    )
```

```python
import jax
import jax.numpy as jnp
from jax import lax
from jax.sharding import PartitionSpec as P


def with_halo(cells, sides, width):
    for axis, dim in sides:
        count = lax.axis_size(axis)
        ends = count - 1
        head = lax.slice_in_dim(cells, 0, width, axis=dim)
        tail = lax.slice_in_dim(cells, cells.shape[dim] - width, cells.shape[dim], axis=dim)
        cells = jnp.concatenate(
            [
                lax.ppermute(tail, axis, [(i, (i + 1) % count) for i in range(ends)]),
                cells,
                lax.ppermute(head, axis, [((i + 1) % count, i) for i in range(ends)]),
            ],
            axis=dim,
        )
    return cells


def device_bits():
    bits = []
    for axis in ("coarse", "sub"):
        size = lax.axis_size(axis)
        mask = 1
        while mask < size:
            bits.append((axis, mask))
            mask *= 2
        assert mask == size
    return bits


def bit_of(axis, mask):
    return (lax.axis_index(axis) // mask) % 2


def pairs(axis, mask):
    return [(i, i ^ mask) for i in range(lax.axis_size(axis))]


def halve(x, dim, axis, mask, wire):
    v = bit_of(axis, mask)
    keep = lax.dynamic_index_in_dim(x, v, axis=dim, keepdims=True)
    send = lax.dynamic_index_in_dim(x, 1 - v, axis=dim, keepdims=True)
    return keep + lax.ppermute(send.astype(wire), axis, pairs(axis, mask)).astype(x.dtype)


def double(y, dim, axis, mask):
    v = bit_of(axis, mask)
    recv = lax.ppermute(y, axis, pairs(axis, mask))
    return jnp.where(v == 0, jnp.concatenate([y, recv], axis=dim), jnp.concatenate([recv, y], axis=dim))


def stream_orders(nbits, streams):
    rest = list(range(1, nbits))
    orders = []
    for s in range(streams):
        k = (s * len(rest)) // streams
        orders.append([0] + rest[k:] + rest[:k])
    return orders


def per_device(residual, margin, inverse_blocks, interface, basis, coarse_pattern, coarse_inverse):
    rows, cols = coarse_inverse.shape[-2:]
    tags = jnp.broadcast_to(coarse_pattern.astype(jnp.bfloat16)[:, :, None, None], coarse_pattern.shape + (8, cols))
    packed = lax.all_gather(jnp.concatenate([coarse_inverse, tags], axis=2), "coarse", axis=0, tiled=True)
    inverse_all = packed[:, :, :rows, :]
    pattern_all = packed[:, :, rows, 0].astype(jnp.int32)
    extended = with_halo(residual, ((("sub", "coarse"), 0),), 1)
    rhs = residual.shape[1]
    width = basis.shape[-1]
    total_blocks = pattern_all.shape[0]
    terms = jnp.einsum("jrb,jqbc->jqrc", residual, basis, preferred_element_type=jnp.float32)
    labels = jnp.arange(total_blocks, dtype=jnp.int32)
    onehot = (interface[:, :, None] == labels[None, None, :]).astype(jnp.float32)
    restricted = jnp.einsum("jqn,jqrc->nrc", onehot, terms, precision=lax.Precision.HIGHEST)

    bits = device_bits()
    nb = len(bits)
    inner = rhs >> nb
    assert inner << nb == rhs
    streams = 3 if total_blocks % 3 == 0 else 1
    per = total_blocks // streams
    orders = stream_orders(nb, streams)
    split = restricted.reshape((total_blocks,) + (2,) * nb + (inner, width))
    parts = [lax.slice_in_dim(split, s * per, (s + 1) * per, axis=0) for s in range(streams)]
    picked = jnp.take(extended, margin, axis=0)
    local = jnp.einsum("jerb,jebc->jrc", picked, inverse_blocks, preferred_element_type=jnp.float32)
    for step in range(nb):
        wire = jnp.float32
        parts = [halve(x, 1 + orders[s][step], *bits[orders[s][step]], wire) for s, x in enumerate(parts)]
        if step == 0:
            local, parts = lax.optimization_barrier((local, parts))
    mine = jnp.concatenate(parts, axis=0).reshape(total_blocks, inner, width)
    coarse_in = mine.astype(jnp.bfloat16)
    chosen = jnp.take(coarse_in, pattern_all, axis=0)
    solved = jnp.einsum(
        "nerc,necd->nrd", chosen, inverse_all, preferred_element_type=jnp.float32
    ).astype(jnp.bfloat16)
    solved = solved.reshape((total_blocks,) + (1,) * nb + (inner, width))
    outs = [lax.slice_in_dim(solved, s * per, (s + 1) * per, axis=0) for s in range(streams)]
    for step in reversed(range(nb)):
        outs = [double(y, 1 + orders[s][step], *bits[orders[s][step]]) for s, y in enumerate(outs)]
    coarse_out = jnp.concatenate(outs, axis=0).reshape(total_blocks, rhs, width)

    lifted = jnp.take(coarse_out, interface, axis=0)
    spread = jnp.einsum("jqrc,jqbc->jrb", lifted, basis, preferred_element_type=jnp.float32)
    return (local + spread).astype(jnp.bfloat16)


def solution(mesh):
    in_specs = (
        P(("sub", "coarse"), None, None),
        P(("sub", "coarse"), None),
        P(("sub", "coarse"), None, None, None),
        P(("sub", "coarse"), None),
        P(("sub", "coarse"), None, None, None),
        P("coarse", None),
        P("coarse", None, None, None),
    )
    out_specs = P(("sub", "coarse"), None, None)
    return jax.shard_map(
        per_device, mesh=mesh, in_specs=in_specs, out_specs=out_specs, check_vma=False
    )
```

```python
import jax
import jax.numpy as jnp
from jax import lax
from jax.sharding import PartitionSpec as P


def with_halo(cells, sides, width):
    for axis, dim in sides:
        count = lax.axis_size(axis)
        ends = count - 1
        head = lax.slice_in_dim(cells, 0, width, axis=dim)
        tail = lax.slice_in_dim(cells, cells.shape[dim] - width, cells.shape[dim], axis=dim)
        cells = jnp.concatenate(
            [
                lax.ppermute(tail, axis, [(i, (i + 1) % count) for i in range(ends)]),
                cells,
                lax.ppermute(head, axis, [((i + 1) % count, i) for i in range(ends)]),
            ],
            axis=dim,
        )
    return cells


def device_bits():
    bits = []
    for axis in ("coarse", "sub"):
        size = lax.axis_size(axis)
        mask = 1
        while mask < size:
            bits.append((axis, mask))
            mask *= 2
        assert mask == size
    return bits


def bit_of(axis, mask):
    return (lax.axis_index(axis) // mask) % 2


def pairs(axis, mask):
    return [(i, i ^ mask) for i in range(lax.axis_size(axis))]


def halve(x, dim, axis, mask, wire):
    v = bit_of(axis, mask)
    keep = lax.dynamic_index_in_dim(x, v, axis=dim, keepdims=True)
    send = lax.dynamic_index_in_dim(x, 1 - v, axis=dim, keepdims=True)
    return keep + lax.ppermute(send.astype(wire), axis, pairs(axis, mask)).astype(x.dtype)


def double(y, dim, axis, mask):
    v = bit_of(axis, mask)
    recv = lax.ppermute(y, axis, pairs(axis, mask))
    return jnp.where(v == 0, jnp.concatenate([y, recv], axis=dim), jnp.concatenate([recv, y], axis=dim))


def stream_orders(nbits, streams):
    rest = list(range(1, nbits))
    orders = []
    for s in range(streams):
        k = (s * len(rest)) // streams
        orders.append([0] + rest[k:] + rest[:k])
    return orders


def per_device(residual, margin, inverse_blocks, interface, basis, coarse_pattern, coarse_inverse):
    rows, cols = coarse_inverse.shape[-2:]
    tags = jnp.broadcast_to(coarse_pattern.astype(jnp.bfloat16)[:, :, None, None], coarse_pattern.shape + (8, cols))
    packed = lax.all_gather(jnp.concatenate([coarse_inverse, tags], axis=2), "coarse", axis=0, tiled=True)
    inverse_all = packed[:, :, :rows, :]
    pattern_all = packed[:, :, rows, 0].astype(jnp.int32)
    extended = with_halo(residual, ((("sub", "coarse"), 0),), 1)
    rhs = residual.shape[1]
    width = basis.shape[-1]
    total_blocks = pattern_all.shape[0]
    terms = jnp.einsum("jrb,jqbc->jqrc", residual, basis, preferred_element_type=jnp.float32)
    labels = jnp.arange(total_blocks, dtype=jnp.int32)
    onehot = (interface[:, :, None] == labels[None, None, :]).astype(jnp.float32)
    restricted = jnp.einsum("jqn,jqrc->nrc", onehot, terms, precision=lax.Precision.HIGHEST)

    bits = device_bits()
    nb = len(bits)
    inner = rhs >> nb
    assert inner << nb == rhs
    streams = 3 if total_blocks % 3 == 0 else 1
    per = total_blocks // streams
    orders = stream_orders(nb, streams)
    split = restricted.reshape((total_blocks,) + (2,) * nb + (inner, width))
    parts = [lax.slice_in_dim(split, s * per, (s + 1) * per, axis=0) for s in range(streams)]
    picked = jnp.take(extended, margin, axis=0)
    local = jnp.einsum("jerb,jebc->jrc", picked, inverse_blocks, preferred_element_type=jnp.float32)
    for step in range(nb):
        wire = jnp.bfloat16 if step in (1, 2) else jnp.float32
        parts = [halve(x, 1 + orders[s][step], *bits[orders[s][step]], wire) for s, x in enumerate(parts)]
        if step == 0:
            local, parts = lax.optimization_barrier((local, parts))
    mine = jnp.concatenate(parts, axis=0).reshape(total_blocks, inner, width)
    coarse_in = mine.astype(jnp.bfloat16)
    chosen = jnp.take(coarse_in, pattern_all, axis=0)
    solved = jnp.einsum(
        "nerc,necd->nrd", chosen, inverse_all, preferred_element_type=jnp.float32
    ).astype(jnp.bfloat16)
    solved = solved.reshape((total_blocks,) + (1,) * nb + (inner, width))
    outs = [lax.slice_in_dim(solved, s * per, (s + 1) * per, axis=0) for s in range(streams)]
    for step in reversed(range(nb)):
        outs = [double(y, 1 + orders[s][step], *bits[orders[s][step]]) for s, y in enumerate(outs)]
    coarse_out = jnp.concatenate(outs, axis=0).reshape(total_blocks, rhs, width)

    lifted = jnp.take(coarse_out, interface, axis=0)
    spread = jnp.einsum("jqrc,jqbc->jrb", lifted, basis, preferred_element_type=jnp.float32)
    return (local + spread).astype(jnp.bfloat16)


def solution(mesh):
    in_specs = (
        P(("sub", "coarse"), None, None),
        P(("sub", "coarse"), None),
        P(("sub", "coarse"), None, None, None),
        P(("sub", "coarse"), None),
        P(("sub", "coarse"), None, None, None),
        P("coarse", None),
        P("coarse", None, None, None),
    )
    out_specs = P(("sub", "coarse"), None, None)
    return jax.shard_map(
        per_device, mesh=mesh, in_specs=in_specs, out_specs=out_specs, check_vma=False
    )
```

```python
import jax
import jax.numpy as jnp
from jax import lax
from jax.sharding import PartitionSpec as P


def with_halo(cells, sides, width):
    for axis, dim in sides:
        count = lax.axis_size(axis)
        ends = count - 1
        head = lax.slice_in_dim(cells, 0, width, axis=dim)
        tail = lax.slice_in_dim(cells, cells.shape[dim] - width, cells.shape[dim], axis=dim)
        cells = jnp.concatenate(
            [
                lax.ppermute(tail, axis, [(i, (i + 1) % count) for i in range(ends)]),
                cells,
                lax.ppermute(head, axis, [((i + 1) % count, i) for i in range(ends)]),
            ],
            axis=dim,
        )
    return cells


def device_bits():
    bits = []
    for axis in ("coarse", "sub"):
        size = lax.axis_size(axis)
        mask = 1
        while mask < size:
            bits.append((axis, mask))
            mask *= 2
        assert mask == size
    return bits


def bit_of(axis, mask):
    return (lax.axis_index(axis) // mask) % 2


def pairs(axis, mask):
    return [(i, i ^ mask) for i in range(lax.axis_size(axis))]


def halve(x, dim, axis, mask, wire):
    v = bit_of(axis, mask)
    keep = lax.dynamic_index_in_dim(x, v, axis=dim, keepdims=True)
    send = lax.dynamic_index_in_dim(x, 1 - v, axis=dim, keepdims=True)
    return keep + lax.ppermute(send.astype(wire), axis, pairs(axis, mask)).astype(x.dtype)


def double(y, dim, axis, mask):
    v = bit_of(axis, mask)
    recv = lax.ppermute(y, axis, pairs(axis, mask))
    return jnp.where(v == 0, jnp.concatenate([y, recv], axis=dim), jnp.concatenate([recv, y], axis=dim))


def stream_orders(nbits, streams):
    rest = list(range(1, nbits))
    orders = []
    for s in range(streams):
        k = (s * len(rest)) // streams
        orders.append([0] + rest[k:] + rest[:k])
    return orders


def per_device(residual, margin, inverse_blocks, interface, basis, coarse_pattern, coarse_inverse):
    rows, cols = coarse_inverse.shape[-2:]
    tags = jnp.broadcast_to(coarse_pattern.astype(jnp.bfloat16)[:, :, None, None], coarse_pattern.shape + (8, cols))
    packed = lax.all_gather(jnp.concatenate([coarse_inverse, tags], axis=2), "coarse", axis=0, tiled=True)
    inverse_all = packed[:, :, :rows, :]
    pattern_all = packed[:, :, rows, 0].astype(jnp.int32)
    extended = with_halo(residual, ((("sub", "coarse"), 0),), 1)
    rhs = residual.shape[1]
    width = basis.shape[-1]
    total_blocks = pattern_all.shape[0]
    terms = jnp.einsum("jrb,jqbc->jqrc", residual, basis, preferred_element_type=jnp.float32)
    labels = jnp.arange(total_blocks, dtype=jnp.int32)
    onehot = (interface[:, :, None] == labels[None, None, :]).astype(jnp.float32)
    restricted = jnp.einsum("jqn,jqrc->nrc", onehot, terms, precision=lax.Precision.HIGHEST)

    bits = device_bits()
    nb = len(bits)
    inner = rhs >> nb
    assert inner << nb == rhs
    streams = 3 if total_blocks % 3 == 0 else 1
    per = total_blocks // streams
    orders = stream_orders(nb, streams)
    split = restricted.reshape((total_blocks,) + (2,) * nb + (inner, width))
    whole = halve(split, 1, *bits[0], jnp.float32)
    extended, inverse_blocks, whole = lax.optimization_barrier((extended, inverse_blocks, whole))
    parts = [lax.slice_in_dim(whole, s * per, (s + 1) * per, axis=0) for s in range(streams)]
    picked = jnp.take(extended, margin, axis=0)
    local = jnp.einsum("jerb,jebc->jrc", picked, inverse_blocks, preferred_element_type=jnp.float32)
    for step in range(1, nb):
        parts = [halve(x, 1 + orders[s][step], *bits[orders[s][step]], jnp.float32) for s, x in enumerate(parts)]
        if step == 1:
            local, parts = lax.optimization_barrier((local, parts))
    mine = jnp.concatenate(parts, axis=0).reshape(total_blocks, inner, width)
    coarse_in = mine.astype(jnp.bfloat16)
    chosen = jnp.take(coarse_in, pattern_all, axis=0)
    solved = jnp.einsum(
        "nerc,necd->nrd", chosen, inverse_all, preferred_element_type=jnp.float32
    ).astype(jnp.bfloat16)
    solved = solved.reshape((total_blocks,) + (1,) * nb + (inner, width))
    outs = [lax.slice_in_dim(solved, s * per, (s + 1) * per, axis=0) for s in range(streams)]
    for step in reversed(range(1, nb)):
        outs = [double(y, 1 + orders[s][step], *bits[orders[s][step]]) for s, y in enumerate(outs)]
    coarse_out = double(jnp.concatenate(outs, axis=0), 1, *bits[0])
    coarse_out = coarse_out.reshape(total_blocks, rhs, width)

    lifted = jnp.take(coarse_out, interface, axis=0)
    spread = jnp.einsum("jqrc,jqbc->jrb", lifted, basis, preferred_element_type=jnp.float32)
    return (local + spread).astype(jnp.bfloat16)


def solution(mesh):
    in_specs = (
        P(("sub", "coarse"), None, None),
        P(("sub", "coarse"), None),
        P(("sub", "coarse"), None, None, None),
        P(("sub", "coarse"), None),
        P(("sub", "coarse"), None, None, None),
        P("coarse", None),
        P("coarse", None, None, None),
    )
    out_specs = P(("sub", "coarse"), None, None)
    return jax.shard_map(
        per_device, mesh=mesh, in_specs=in_specs, out_specs=out_specs, check_vma=False
    )
```

```python
import jax
import jax.numpy as jnp
from jax import lax
from jax.experimental import pallas as pl
from jax.experimental.pallas import tpu as pltpu
from jax.sharding import PartitionSpec as P


def restrict_kernel(links, residual_ref, basis_ref, out_ref):
    j = pl.program_id(0)
    q = pl.program_id(1)

    @pl.when((j == 0) & (q == 0))
    def _():
        out_ref[...] = jnp.zeros_like(out_ref)

    n = links[j, q]
    out_ref[n] += jnp.dot(residual_ref[0], basis_ref[0, 0], preferred_element_type=jnp.float32)


def restrict(residual, basis, interface, total_blocks):
    count, rhs, size = residual.shape
    width = basis.shape[-1]
    return pl.pallas_call(
        restrict_kernel,
        out_shape=jax.ShapeDtypeStruct((total_blocks, rhs, width), jnp.float32),
        grid_spec=pltpu.PrefetchScalarGridSpec(
            num_scalar_prefetch=1,
            grid=(count, interface.shape[1]),
            in_specs=[
                pl.BlockSpec((1, rhs, size), lambda j, q, links: (j, 0, 0)),
                pl.BlockSpec((1, 1, size, width), lambda j, q, links: (j, q, 0, 0)),
            ],
            out_specs=pl.BlockSpec((total_blocks, rhs, width), lambda j, q, links: (0, 0, 0)),
        ),
        compiler_params=pltpu.CompilerParams(dimension_semantics=("arbitrary", "arbitrary")),
        cost_estimate=pl.CostEstimate(
            flops=2 * count * interface.shape[1] * rhs * size * width,
            bytes_accessed=residual.size * 2 + basis.size * 2 + total_blocks * rhs * width * 4,
            transcendentals=0,
        ),
    )(interface, residual, basis)


def with_halo(cells, sides, width):
    for axis, dim in sides:
        count = lax.axis_size(axis)
        ends = count - 1
        head = lax.slice_in_dim(cells, 0, width, axis=dim)
        tail = lax.slice_in_dim(cells, cells.shape[dim] - width, cells.shape[dim], axis=dim)
        cells = jnp.concatenate(
            [
                lax.ppermute(tail, axis, [(i, (i + 1) % count) for i in range(ends)]),
                cells,
                lax.ppermute(head, axis, [((i + 1) % count, i) for i in range(ends)]),
            ],
            axis=dim,
        )
    return cells


def device_bits():
    bits = []
    for axis in ("coarse", "sub"):
        size = lax.axis_size(axis)
        mask = 1
        while mask < size:
            bits.append((axis, mask))
            mask *= 2
        assert mask == size
    return bits


def bit_of(axis, mask):
    return (lax.axis_index(axis) // mask) % 2


def pairs(axis, mask):
    return [(i, i ^ mask) for i in range(lax.axis_size(axis))]


def halve(x, dim, axis, mask, wire):
    v = bit_of(axis, mask)
    keep = lax.dynamic_index_in_dim(x, v, axis=dim, keepdims=True)
    send = lax.dynamic_index_in_dim(x, 1 - v, axis=dim, keepdims=True)
    return keep + lax.ppermute(send.astype(wire), axis, pairs(axis, mask)).astype(x.dtype)


def double(y, dim, axis, mask):
    v = bit_of(axis, mask)
    recv = lax.ppermute(y, axis, pairs(axis, mask))
    return jnp.where(v == 0, jnp.concatenate([y, recv], axis=dim), jnp.concatenate([recv, y], axis=dim))


def stream_orders(nbits, streams):
    rest = list(range(1, nbits))
    orders = []
    for s in range(streams):
        k = (s * len(rest)) // streams
        orders.append([0] + rest[k:] + rest[:k])
    return orders


def per_device(residual, margin, inverse_blocks, interface, basis, coarse_pattern, coarse_inverse):
    rows, cols = coarse_inverse.shape[-2:]
    tags = jnp.broadcast_to(coarse_pattern.astype(jnp.bfloat16)[:, :, None, None], coarse_pattern.shape + (8, cols))
    packed = lax.all_gather(jnp.concatenate([coarse_inverse, tags], axis=2), "coarse", axis=0, tiled=True)
    inverse_all = packed[:, :, :rows, :]
    pattern_all = packed[:, :, rows, 0].astype(jnp.int32)
    extended = with_halo(residual, ((("sub", "coarse"), 0),), 1)
    rhs = residual.shape[1]
    width = basis.shape[-1]
    total_blocks = pattern_all.shape[0]
    restricted = restrict(residual, basis, interface, total_blocks)

    bits = device_bits()
    nb = len(bits)
    inner = rhs >> nb
    assert inner << nb == rhs
    streams = 3 if total_blocks % 3 == 0 else 1
    per = total_blocks // streams
    orders = stream_orders(nb, streams)
    split = restricted.reshape((total_blocks,) + (2,) * nb + (inner, width))
    whole = halve(split, 1, *bits[0], jnp.float32)
    extended, inverse_blocks, whole = lax.optimization_barrier((extended, inverse_blocks, whole))
    parts = [lax.slice_in_dim(whole, s * per, (s + 1) * per, axis=0) for s in range(streams)]
    picked = jnp.take(extended, margin, axis=0)
    local = jnp.einsum("jerb,jebc->jrc", picked, inverse_blocks, preferred_element_type=jnp.float32)
    for step in range(1, nb):
        parts = [halve(x, 1 + orders[s][step], *bits[orders[s][step]], jnp.float32) for s, x in enumerate(parts)]
        if step == 1:
            local, parts = lax.optimization_barrier((local, parts))
    mine = jnp.concatenate(parts, axis=0).reshape(total_blocks, inner, width)
    coarse_in = mine.astype(jnp.bfloat16)
    chosen = jnp.take(coarse_in, pattern_all, axis=0)
    solved = jnp.einsum(
        "nerc,necd->nrd", chosen, inverse_all, preferred_element_type=jnp.float32
    ).astype(jnp.bfloat16)
    solved = solved.reshape((total_blocks,) + (1,) * nb + (inner, width))
    outs = [lax.slice_in_dim(solved, s * per, (s + 1) * per, axis=0) for s in range(streams)]
    for step in reversed(range(1, nb)):
        outs = [double(y, 1 + orders[s][step], *bits[orders[s][step]]) for s, y in enumerate(outs)]
    coarse_out = double(jnp.concatenate(outs, axis=0), 1, *bits[0])
    coarse_out = coarse_out.reshape(total_blocks, rhs, width)

    lifted = jnp.take(coarse_out, interface, axis=0)
    spread = jnp.einsum("jqrc,jqbc->jrb", lifted, basis, preferred_element_type=jnp.float32)
    return (local + spread).astype(jnp.bfloat16)


def solution(mesh):
    in_specs = (
        P(("sub", "coarse"), None, None),
        P(("sub", "coarse"), None),
        P(("sub", "coarse"), None, None, None),
        P(("sub", "coarse"), None),
        P(("sub", "coarse"), None, None, None),
        P("coarse", None),
        P("coarse", None, None, None),
    )
    out_specs = P(("sub", "coarse"), None, None)
    return jax.shard_map(
        per_device, mesh=mesh, in_specs=in_specs, out_specs=out_specs, check_vma=False
    )
```

```python
import jax
import jax.numpy as jnp
from jax import lax
from jax.experimental import pallas as pl
from jax.experimental.pallas import tpu as pltpu
from jax.sharding import PartitionSpec as P


def restrict_kernel(links, half, residual_ref, basis_ref, keep_ref, send_ref):
    j = pl.program_id(0)
    q = pl.program_id(1)

    @pl.when((j == 0) & (q == 0))
    def _():
        keep_ref[...] = jnp.zeros_like(keep_ref)
        send_ref[...] = jnp.zeros_like(send_ref)

    n = links[j, q]
    rows = keep_ref.shape[1]
    mine = pl.multiple_of(half[0] * rows, rows)
    other = pl.multiple_of((1 - half[0]) * rows, rows)
    keep_ref[n] += jnp.dot(residual_ref[0, pl.ds(mine, rows), :], basis_ref[0, 0], preferred_element_type=jnp.float32)
    send_ref[n] += jnp.dot(residual_ref[0, pl.ds(other, rows), :], basis_ref[0, 0], preferred_element_type=jnp.float32)


def restrict(residual, basis, interface, total_blocks, half):
    count, rhs, size = residual.shape
    width = basis.shape[-1]
    rows = rhs // 2
    block = pl.BlockSpec((total_blocks, rows, width), lambda j, q, links, half: (0, 0, 0))
    return pl.pallas_call(
        restrict_kernel,
        out_shape=[jax.ShapeDtypeStruct((total_blocks, rows, width), jnp.float32)] * 2,
        grid_spec=pltpu.PrefetchScalarGridSpec(
            num_scalar_prefetch=2,
            grid=(count, interface.shape[1]),
            in_specs=[
                pl.BlockSpec((1, rhs, size), lambda j, q, links, half: (j, 0, 0)),
                pl.BlockSpec((1, 1, size, width), lambda j, q, links, half: (j, q, 0, 0)),
            ],
            out_specs=[block, block],
        ),
        compiler_params=pltpu.CompilerParams(dimension_semantics=("arbitrary", "arbitrary")),
        cost_estimate=pl.CostEstimate(
            flops=2 * count * interface.shape[1] * rhs * size * width,
            bytes_accessed=residual.size * 2 + basis.size * 2 + total_blocks * rhs * width * 4,
            transcendentals=0,
        ),
    )(interface, half, residual, basis)


def with_halo(cells, sides, width):
    for axis, dim in sides:
        count = lax.axis_size(axis)
        ends = count - 1
        head = lax.slice_in_dim(cells, 0, width, axis=dim)
        tail = lax.slice_in_dim(cells, cells.shape[dim] - width, cells.shape[dim], axis=dim)
        cells = jnp.concatenate(
            [
                lax.ppermute(tail, axis, [(i, (i + 1) % count) for i in range(ends)]),
                cells,
                lax.ppermute(head, axis, [((i + 1) % count, i) for i in range(ends)]),
            ],
            axis=dim,
        )
    return cells


def device_bits():
    bits = []
    for axis in ("coarse", "sub"):
        size = lax.axis_size(axis)
        mask = 1
        while mask < size:
            bits.append((axis, mask))
            mask *= 2
        assert mask == size
    return bits


def bit_of(axis, mask):
    return (lax.axis_index(axis) // mask) % 2


def pairs(axis, mask):
    return [(i, i ^ mask) for i in range(lax.axis_size(axis))]


def halve(x, dim, axis, mask, wire):
    v = bit_of(axis, mask)
    keep = lax.dynamic_index_in_dim(x, v, axis=dim, keepdims=True)
    send = lax.dynamic_index_in_dim(x, 1 - v, axis=dim, keepdims=True)
    return keep + lax.ppermute(send.astype(wire), axis, pairs(axis, mask)).astype(x.dtype)


def double(y, dim, axis, mask):
    v = bit_of(axis, mask)
    recv = lax.ppermute(y, axis, pairs(axis, mask))
    return jnp.where(v == 0, jnp.concatenate([y, recv], axis=dim), jnp.concatenate([recv, y], axis=dim))


def stream_orders(nbits, streams):
    rest = list(range(1, nbits))
    orders = []
    for s in range(streams):
        k = (s * len(rest)) // streams
        orders.append([0] + rest[k:] + rest[:k])
    return orders


def per_device(residual, margin, inverse_blocks, interface, basis, coarse_pattern, coarse_inverse):
    rows, cols = coarse_inverse.shape[-2:]
    tags = jnp.broadcast_to(coarse_pattern.astype(jnp.bfloat16)[:, :, None, None], coarse_pattern.shape + (8, cols))
    packed = lax.all_gather(jnp.concatenate([coarse_inverse, tags], axis=2), "coarse", axis=0, tiled=True)
    inverse_all = packed[:, :, :rows, :]
    pattern_all = packed[:, :, rows, 0].astype(jnp.int32)
    extended = with_halo(residual, ((("sub", "coarse"), 0),), 1)
    rhs = residual.shape[1]
    width = basis.shape[-1]
    total_blocks = pattern_all.shape[0]
    bits = device_bits()
    own_half = bit_of(*bits[0])
    keep, send = restrict(residual, basis, interface, total_blocks, own_half.reshape(1).astype(jnp.int32))

    nb = len(bits)
    inner = rhs >> nb
    assert inner << nb == rhs
    streams = 3 if total_blocks % 3 == 0 else 1
    per = total_blocks // streams
    orders = stream_orders(nb, streams)
    whole = keep + lax.ppermute(send, bits[0][0], pairs(*bits[0]))
    whole = whole.reshape((total_blocks, 1) + (2,) * (nb - 1) + (inner, width))
    extended, inverse_blocks, whole = lax.optimization_barrier((extended, inverse_blocks, whole))
    parts = [lax.slice_in_dim(whole, s * per, (s + 1) * per, axis=0) for s in range(streams)]
    picked = jnp.take(extended, margin, axis=0)
    local = jnp.einsum("jerb,jebc->jrc", picked, inverse_blocks, preferred_element_type=jnp.float32)
    for step in range(1, nb):
        parts = [halve(x, 1 + orders[s][step], *bits[orders[s][step]], jnp.float32) for s, x in enumerate(parts)]
        if step == 1:
            local, parts = lax.optimization_barrier((local, parts))
    mine = jnp.concatenate(parts, axis=0).reshape(total_blocks, inner, width)
    coarse_in = mine.astype(jnp.bfloat16)
    chosen = jnp.take(coarse_in, pattern_all, axis=0)
    solved = jnp.einsum(
        "nerc,necd->nrd", chosen, inverse_all, preferred_element_type=jnp.float32
    ).astype(jnp.bfloat16)
    solved = solved.reshape((total_blocks,) + (1,) * nb + (inner, width))
    outs = [lax.slice_in_dim(solved, s * per, (s + 1) * per, axis=0) for s in range(streams)]
    for step in reversed(range(1, nb)):
        outs = [double(y, 1 + orders[s][step], *bits[orders[s][step]]) for s, y in enumerate(outs)]
    own = jnp.concatenate(outs, axis=0).reshape(total_blocks, rhs // 2, width)
    got = lax.ppermute(own, bits[0][0], pairs(*bits[0]))
    own_rows = jnp.take(own, interface, axis=0)
    got_rows = jnp.take(got, interface, axis=0)
    lifted = jnp.where(
        own_half == 0,
        jnp.concatenate([own_rows, got_rows], axis=2),
        jnp.concatenate([got_rows, own_rows], axis=2),
    )

    spread = jnp.einsum("jqrc,jqbc->jrb", lifted, basis, preferred_element_type=jnp.float32)
    return (local + spread).astype(jnp.bfloat16)


def solution(mesh):
    in_specs = (
        P(("sub", "coarse"), None, None),
        P(("sub", "coarse"), None),
        P(("sub", "coarse"), None, None, None),
        P(("sub", "coarse"), None),
        P(("sub", "coarse"), None, None, None),
        P("coarse", None),
        P("coarse", None, None, None),
    )
    out_specs = P(("sub", "coarse"), None, None)
    return jax.shard_map(
        per_device, mesh=mesh, in_specs=in_specs, out_specs=out_specs, check_vma=False
    )
```

```python
import jax
import jax.numpy as jnp
from jax import lax
from jax.experimental import pallas as pl
from jax.experimental.pallas import tpu as pltpu
from jax.sharding import PartitionSpec as P


def restrict_kernel(links, half, residual_ref, basis_ref, keep_ref, send_ref):
    j = pl.program_id(0)
    pairs_per = basis_ref.shape[1]
    rows = keep_ref.shape[1]

    @pl.when(j == 0)
    def _():
        keep_ref[...] = jnp.zeros_like(keep_ref)
        send_ref[...] = jnp.zeros_like(send_ref)

    for q in range(pairs_per):
        n = links[j * pairs_per + q]
        term = jnp.dot(residual_ref[0], basis_ref[0, q], preferred_element_type=jnp.float32)

        @pl.when(half[0] == 0)
        def _():
            keep_ref[n] += term[:rows]
            send_ref[n] += term[rows:]

        @pl.when(half[0] != 0)
        def _():
            keep_ref[n] += term[rows:]
            send_ref[n] += term[:rows]


def restrict(residual, basis, interface, total_blocks, half):
    count, rhs, size = residual.shape
    width = basis.shape[-1]
    rows = rhs // 2
    block = pl.BlockSpec((total_blocks, rows, width), lambda j, links, half: (0, 0, 0))
    return pl.pallas_call(
        restrict_kernel,
        out_shape=[jax.ShapeDtypeStruct((total_blocks, rows, width), jnp.float32)] * 2,
        grid_spec=pltpu.PrefetchScalarGridSpec(
            num_scalar_prefetch=2,
            grid=(count,),
            in_specs=[
                pl.BlockSpec((1, rhs, size), lambda j, links, half: (j, 0, 0)),
                pl.BlockSpec((1, interface.shape[1], size, width), lambda j, links, half: (j, 0, 0, 0)),
            ],
            out_specs=[block, block],
        ),
        compiler_params=pltpu.CompilerParams(dimension_semantics=("arbitrary",)),
        cost_estimate=pl.CostEstimate(
            flops=2 * count * interface.shape[1] * rhs * size * width,
            bytes_accessed=residual.size * 2 + basis.size * 2 + total_blocks * rhs * width * 4,
            transcendentals=0,
        ),
    )(interface.reshape(-1), half, residual, basis)


def with_halo(cells, sides, width):
    for axis, dim in sides:
        count = lax.axis_size(axis)
        ends = count - 1
        head = lax.slice_in_dim(cells, 0, width, axis=dim)
        tail = lax.slice_in_dim(cells, cells.shape[dim] - width, cells.shape[dim], axis=dim)
        cells = jnp.concatenate(
            [
                lax.ppermute(tail, axis, [(i, (i + 1) % count) for i in range(ends)]),
                cells,
                lax.ppermute(head, axis, [((i + 1) % count, i) for i in range(ends)]),
            ],
            axis=dim,
        )
    return cells


def device_bits():
    bits = []
    for axis in ("coarse", "sub"):
        size = lax.axis_size(axis)
        mask = 1
        while mask < size:
            bits.append((axis, mask))
            mask *= 2
        assert mask == size
    return bits


def bit_of(axis, mask):
    return (lax.axis_index(axis) // mask) % 2


def pairs(axis, mask):
    return [(i, i ^ mask) for i in range(lax.axis_size(axis))]


def halve(x, dim, axis, mask, wire):
    v = bit_of(axis, mask)
    keep = lax.dynamic_index_in_dim(x, v, axis=dim, keepdims=True)
    send = lax.dynamic_index_in_dim(x, 1 - v, axis=dim, keepdims=True)
    return keep + lax.ppermute(send.astype(wire), axis, pairs(axis, mask)).astype(x.dtype)


def double(y, dim, axis, mask):
    v = bit_of(axis, mask)
    recv = lax.ppermute(y, axis, pairs(axis, mask))
    return jnp.where(v == 0, jnp.concatenate([y, recv], axis=dim), jnp.concatenate([recv, y], axis=dim))


def stream_orders(nbits, streams):
    rest = list(range(1, nbits))
    orders = []
    for s in range(streams):
        k = (s * len(rest)) // streams
        orders.append([0] + rest[k:] + rest[:k])
    return orders


def per_device(residual, margin, inverse_blocks, interface, basis, coarse_pattern, coarse_inverse):
    rows, cols = coarse_inverse.shape[-2:]
    tags = jnp.broadcast_to(coarse_pattern.astype(jnp.bfloat16)[:, :, None, None], coarse_pattern.shape + (8, cols))
    packed = lax.all_gather(jnp.concatenate([coarse_inverse, tags], axis=2), "coarse", axis=0, tiled=True)
    inverse_all = packed[:, :, :rows, :]
    pattern_all = packed[:, :, rows, 0].astype(jnp.int32)
    extended = with_halo(residual, ((("sub", "coarse"), 0),), 1)
    rhs = residual.shape[1]
    width = basis.shape[-1]
    total_blocks = pattern_all.shape[0]
    bits = device_bits()
    own_half = bit_of(*bits[0])
    keep, send = restrict(residual, basis, interface, total_blocks, own_half.reshape(1).astype(jnp.int32))

    nb = len(bits)
    inner = rhs >> nb
    assert inner << nb == rhs
    streams = 3 if total_blocks % 3 == 0 else 1
    per = total_blocks // streams
    orders = stream_orders(nb, streams)
    whole = keep + lax.ppermute(send, bits[0][0], pairs(*bits[0]))
    whole = whole.reshape((total_blocks, 1) + (2,) * (nb - 1) + (inner, width))
    extended, inverse_blocks, whole = lax.optimization_barrier((extended, inverse_blocks, whole))
    parts = [lax.slice_in_dim(whole, s * per, (s + 1) * per, axis=0) for s in range(streams)]
    picked = jnp.take(extended, margin, axis=0)
    local = jnp.einsum("jerb,jebc->jrc", picked, inverse_blocks, preferred_element_type=jnp.float32)
    for step in range(1, nb):
        parts = [halve(x, 1 + orders[s][step], *bits[orders[s][step]], jnp.float32) for s, x in enumerate(parts)]
        if step == 1:
            local, parts = lax.optimization_barrier((local, parts))
    mine = jnp.concatenate(parts, axis=0).reshape(total_blocks, inner, width)
    coarse_in = mine.astype(jnp.bfloat16)
    chosen = jnp.take(coarse_in, pattern_all, axis=0)
    solved = jnp.einsum(
        "nerc,necd->nrd", chosen, inverse_all, preferred_element_type=jnp.float32
    ).astype(jnp.bfloat16)
    solved = solved.reshape((total_blocks,) + (1,) * nb + (inner, width))
    outs = [lax.slice_in_dim(solved, s * per, (s + 1) * per, axis=0) for s in range(streams)]
    for step in reversed(range(1, nb)):
        outs = [double(y, 1 + orders[s][step], *bits[orders[s][step]]) for s, y in enumerate(outs)]
    own = jnp.concatenate(outs, axis=0).reshape(total_blocks, rhs // 2, width)
    got = lax.ppermute(own, bits[0][0], pairs(*bits[0]))
    own_rows = jnp.take(own, interface, axis=0)
    got_rows = jnp.take(got, interface, axis=0)
    lifted = jnp.where(
        own_half == 0,
        jnp.concatenate([own_rows, got_rows], axis=2),
        jnp.concatenate([got_rows, own_rows], axis=2),
    )

    spread = jnp.einsum("jqrc,jqbc->jrb", lifted, basis, preferred_element_type=jnp.float32)
    return (local + spread).astype(jnp.bfloat16)


def solution(mesh):
    in_specs = (
        P(("sub", "coarse"), None, None),
        P(("sub", "coarse"), None),
        P(("sub", "coarse"), None, None, None),
        P(("sub", "coarse"), None),
        P(("sub", "coarse"), None, None, None),
        P("coarse", None),
        P("coarse", None, None, None),
    )
    out_specs = P(("sub", "coarse"), None, None)
    return jax.shard_map(
        per_device, mesh=mesh, in_specs=in_specs, out_specs=out_specs, check_vma=False
    )
```

```python
import functools

import jax
import jax.numpy as jnp
from jax import lax
from jax.experimental import pallas as pl
from jax.experimental.pallas import tpu as pltpu
from jax.sharding import PartitionSpec as P


def restrict_kernel(links, half, residual_ref, basis_ref, out_ref, *, upper):
    j = pl.program_id(0)
    pairs_per = basis_ref.shape[1]
    rows = out_ref.shape[1]

    @pl.when(j == 0)
    def _():
        out_ref[...] = jnp.zeros_like(out_ref)

    for q in range(pairs_per):
        n = links[j * pairs_per + q]

        @pl.when(half[0] == upper)
        def _():
            out_ref[n] += jnp.dot(residual_ref[0, :rows], basis_ref[0, q], preferred_element_type=jnp.float32)

        @pl.when(half[0] != upper)
        def _():
            out_ref[n] += jnp.dot(residual_ref[0, rows:], basis_ref[0, q], preferred_element_type=jnp.float32)


def restrict(residual, basis, links, total_blocks, half, upper):
    count, rhs, size = residual.shape
    width = basis.shape[-1]
    rows = rhs // 2
    return pl.pallas_call(
        functools.partial(restrict_kernel, upper=upper),
        out_shape=jax.ShapeDtypeStruct((total_blocks, rows, width), jnp.float32),
        grid_spec=pltpu.PrefetchScalarGridSpec(
            num_scalar_prefetch=2,
            grid=(count,),
            in_specs=[
                pl.BlockSpec((1, rhs, size), lambda j, links, half: (j, 0, 0)),
                pl.BlockSpec((1, basis.shape[1], size, width), lambda j, links, half: (j, 0, 0, 0)),
            ],
            out_specs=pl.BlockSpec((total_blocks, rows, width), lambda j, links, half: (0, 0, 0)),
        ),
        compiler_params=pltpu.CompilerParams(dimension_semantics=("arbitrary",)),
        cost_estimate=pl.CostEstimate(
            flops=count * basis.shape[1] * rhs * size * width,
            bytes_accessed=residual.size * 2 + basis.size * 2 + total_blocks * rows * width * 4,
            transcendentals=0,
        ),
    )(links, half, residual, basis)


def with_halo(cells, sides, width):
    for axis, dim in sides:
        count = lax.axis_size(axis)
        ends = count - 1
        head = lax.slice_in_dim(cells, 0, width, axis=dim)
        tail = lax.slice_in_dim(cells, cells.shape[dim] - width, cells.shape[dim], axis=dim)
        cells = jnp.concatenate(
            [
                lax.ppermute(tail, axis, [(i, (i + 1) % count) for i in range(ends)]),
                cells,
                lax.ppermute(head, axis, [((i + 1) % count, i) for i in range(ends)]),
            ],
            axis=dim,
        )
    return cells


def device_bits():
    bits = []
    for axis in ("coarse", "sub"):
        size = lax.axis_size(axis)
        mask = 1
        while mask < size:
            bits.append((axis, mask))
            mask *= 2
        assert mask == size
    return bits


def bit_of(axis, mask):
    return (lax.axis_index(axis) // mask) % 2


def pairs(axis, mask):
    return [(i, i ^ mask) for i in range(lax.axis_size(axis))]


def halve(x, dim, axis, mask, wire):
    v = bit_of(axis, mask)
    keep = lax.dynamic_index_in_dim(x, v, axis=dim, keepdims=True)
    send = lax.dynamic_index_in_dim(x, 1 - v, axis=dim, keepdims=True)
    return keep + lax.ppermute(send.astype(wire), axis, pairs(axis, mask)).astype(x.dtype)


def double(y, dim, axis, mask):
    v = bit_of(axis, mask)
    recv = lax.ppermute(y, axis, pairs(axis, mask))
    return jnp.where(v == 0, jnp.concatenate([y, recv], axis=dim), jnp.concatenate([recv, y], axis=dim))


def stream_orders(nbits, streams):
    rest = list(range(1, nbits))
    orders = []
    for s in range(streams):
        k = (s * len(rest)) // streams
        orders.append([0] + rest[k:] + rest[:k])
    return orders


def per_device(residual, margin, inverse_blocks, interface, basis, coarse_pattern, coarse_inverse):
    rows, cols = coarse_inverse.shape[-2:]
    tags = jnp.broadcast_to(coarse_pattern.astype(jnp.bfloat16)[:, :, None, None], coarse_pattern.shape + (8, cols))
    packed = lax.all_gather(jnp.concatenate([coarse_inverse, tags], axis=2), "coarse", axis=0, tiled=True)
    inverse_all = packed[:, :, :rows, :]
    pattern_all = packed[:, :, rows, 0].astype(jnp.int32)
    extended = with_halo(residual, ((("sub", "coarse"), 0),), 1)
    rhs = residual.shape[1]
    width = basis.shape[-1]
    total_blocks = pattern_all.shape[0]
    bits = device_bits()
    own_half = bit_of(*bits[0])
    links = interface.reshape(-1)
    half = own_half.reshape(1).astype(jnp.int32)
    send = restrict(residual, basis, links, total_blocks, half, 1)

    nb = len(bits)
    inner = rhs >> nb
    assert inner << nb == rhs
    streams = 3 if total_blocks % 3 == 0 else 1
    per = total_blocks // streams
    orders = stream_orders(nb, streams)
    got = lax.ppermute(send, bits[0][0], pairs(*bits[0]))
    whole = restrict(residual, basis, links, total_blocks, half, 0) + got
    whole = whole.reshape((total_blocks, 1) + (2,) * (nb - 1) + (inner, width))
    extended, inverse_blocks, whole = lax.optimization_barrier((extended, inverse_blocks, whole))
    parts = [lax.slice_in_dim(whole, s * per, (s + 1) * per, axis=0) for s in range(streams)]
    picked = jnp.take(extended, margin, axis=0)
    local = jnp.einsum("jerb,jebc->jrc", picked, inverse_blocks, preferred_element_type=jnp.float32)
    for step in range(1, nb):
        parts = [halve(x, 1 + orders[s][step], *bits[orders[s][step]], jnp.float32) for s, x in enumerate(parts)]
        if step == 1:
            local, parts = lax.optimization_barrier((local, parts))
    mine = jnp.concatenate(parts, axis=0).reshape(total_blocks, inner, width)
    coarse_in = mine.astype(jnp.bfloat16)
    chosen = jnp.take(coarse_in, pattern_all, axis=0)
    solved = jnp.einsum(
        "nerc,necd->nrd", chosen, inverse_all, preferred_element_type=jnp.float32
    ).astype(jnp.bfloat16)
    solved = solved.reshape((total_blocks,) + (1,) * nb + (inner, width))
    outs = [lax.slice_in_dim(solved, s * per, (s + 1) * per, axis=0) for s in range(streams)]
    for step in reversed(range(1, nb)):
        outs = [double(y, 1 + orders[s][step], *bits[orders[s][step]]) for s, y in enumerate(outs)]
    own = jnp.concatenate(outs, axis=0).reshape(total_blocks, rhs // 2, width)
    got = lax.ppermute(own, bits[0][0], pairs(*bits[0]))
    own_rows = jnp.take(own, interface, axis=0)
    got_rows = jnp.take(got, interface, axis=0)
    lifted = jnp.where(
        own_half == 0,
        jnp.concatenate([own_rows, got_rows], axis=2),
        jnp.concatenate([got_rows, own_rows], axis=2),
    )

    spread = jnp.einsum("jqrc,jqbc->jrb", lifted, basis, preferred_element_type=jnp.float32)
    return (local + spread).astype(jnp.bfloat16)


def solution(mesh):
    in_specs = (
        P(("sub", "coarse"), None, None),
        P(("sub", "coarse"), None),
        P(("sub", "coarse"), None, None, None),
        P(("sub", "coarse"), None),
        P(("sub", "coarse"), None, None, None),
        P("coarse", None),
        P("coarse", None, None, None),
    )
    out_specs = P(("sub", "coarse"), None, None)
    return jax.shard_map(
        per_device, mesh=mesh, in_specs=in_specs, out_specs=out_specs, check_vma=False
    )
```

```python
import functools

import jax
import jax.numpy as jnp
from jax import lax
from jax.experimental import pallas as pl
from jax.experimental.pallas import tpu as pltpu
from jax.sharding import PartitionSpec as P


def restrict_kernel(links, half, residual_ref, basis_ref, out_ref, *, upper):
    j = pl.program_id(0)
    pairs_per = basis_ref.shape[1]
    rows = out_ref.shape[1]

    @pl.when(j == 0)
    def _():
        out_ref[...] = jnp.zeros_like(out_ref)

    for q in range(pairs_per):
        n = links[j * pairs_per + q]

        @pl.when(half[0] == upper)
        def _():
            out_ref[n] += jnp.dot(residual_ref[0, :rows], basis_ref[0, q], preferred_element_type=jnp.float32)

        @pl.when(half[0] != upper)
        def _():
            out_ref[n] += jnp.dot(residual_ref[0, rows:], basis_ref[0, q], preferred_element_type=jnp.float32)


def restrict(residual, basis, links, total_blocks, half, upper):
    count, rhs, size = residual.shape
    width = basis.shape[-1]
    rows = rhs // 2
    return pl.pallas_call(
        functools.partial(restrict_kernel, upper=upper),
        out_shape=jax.ShapeDtypeStruct((total_blocks, rows, width), jnp.float32),
        grid_spec=pltpu.PrefetchScalarGridSpec(
            num_scalar_prefetch=2,
            grid=(count,),
            in_specs=[
                pl.BlockSpec((1, rhs, size), lambda j, links, half: (j, 0, 0)),
                pl.BlockSpec((1, basis.shape[1], size, width), lambda j, links, half: (j, 0, 0, 0)),
            ],
            out_specs=pl.BlockSpec((total_blocks, rows, width), lambda j, links, half: (0, 0, 0)),
        ),
        compiler_params=pltpu.CompilerParams(dimension_semantics=("arbitrary",)),
        cost_estimate=pl.CostEstimate(
            flops=count * basis.shape[1] * rhs * size * width,
            bytes_accessed=residual.size * 2 + basis.size * 2 + total_blocks * rows * width * 4,
            transcendentals=0,
        ),
    )(links, half, residual, basis)


def with_halo(cells, sides, width):
    for axis, dim in sides:
        count = lax.axis_size(axis)
        ends = count - 1
        head = lax.slice_in_dim(cells, 0, width, axis=dim)
        tail = lax.slice_in_dim(cells, cells.shape[dim] - width, cells.shape[dim], axis=dim)
        cells = jnp.concatenate(
            [
                lax.ppermute(tail, axis, [(i, (i + 1) % count) for i in range(ends)]),
                cells,
                lax.ppermute(head, axis, [((i + 1) % count, i) for i in range(ends)]),
            ],
            axis=dim,
        )
    return cells


def device_bits():
    bits = []
    for axis in ("coarse", "sub"):
        size = lax.axis_size(axis)
        mask = 1
        while mask < size:
            bits.append((axis, mask))
            mask *= 2
        assert mask == size
    return bits


def bit_of(axis, mask):
    return (lax.axis_index(axis) // mask) % 2


def pairs(axis, mask):
    return [(i, i ^ mask) for i in range(lax.axis_size(axis))]


def halve(x, dim, axis, mask, wire):
    v = bit_of(axis, mask)
    keep = lax.dynamic_index_in_dim(x, v, axis=dim, keepdims=True)
    send = lax.dynamic_index_in_dim(x, 1 - v, axis=dim, keepdims=True)
    return keep + lax.ppermute(send.astype(wire), axis, pairs(axis, mask)).astype(x.dtype)


def double(y, dim, axis, mask):
    v = bit_of(axis, mask)
    recv = lax.ppermute(y, axis, pairs(axis, mask))
    return jnp.where(v == 0, jnp.concatenate([y, recv], axis=dim), jnp.concatenate([recv, y], axis=dim))


def stream_orders(nbits, streams):
    rest = list(range(1, nbits))
    orders = []
    for s in range(streams):
        k = (s * len(rest)) // streams
        orders.append([0] + rest[k:] + rest[:k])
    return orders


def per_device(residual, margin, inverse_blocks, interface, basis, coarse_pattern, coarse_inverse):
    rows, cols = coarse_inverse.shape[-2:]
    tags = jnp.broadcast_to(coarse_pattern.astype(jnp.bfloat16)[:, :, None, None], coarse_pattern.shape + (8, cols))
    packed = jnp.concatenate([coarse_inverse, tags], axis=2)
    coarse_bits = [bit for bit in device_bits() if bit[0] == "coarse"]
    packed = packed.reshape((1,) * len(coarse_bits) + packed.shape)
    for k in reversed(range(len(coarse_bits))):
        packed = double(packed, len(coarse_bits) - 1 - k, *coarse_bits[k])
    packed = packed.reshape((-1,) + packed.shape[len(coarse_bits) + 1:])
    inverse_all = packed[:, :, :rows, :]
    pattern_all = packed[:, :, rows, 0].astype(jnp.int32)
    extended = with_halo(residual, ((("sub", "coarse"), 0),), 1)
    rhs = residual.shape[1]
    width = basis.shape[-1]
    total_blocks = pattern_all.shape[0]
    bits = device_bits()
    own_half = bit_of(*bits[0])
    links = interface.reshape(-1)
    half = own_half.reshape(1).astype(jnp.int32)
    send = restrict(residual, basis, links, total_blocks, half, 1)

    nb = len(bits)
    inner = rhs >> nb
    assert inner << nb == rhs
    streams = 3 if total_blocks % 3 == 0 else 1
    per = total_blocks // streams
    orders = stream_orders(nb, streams)
    got = lax.ppermute(send, bits[0][0], pairs(*bits[0]))
    whole = restrict(residual, basis, links, total_blocks, half, 0) + got
    whole = whole.reshape((total_blocks, 1) + (2,) * (nb - 1) + (inner, width))
    extended, inverse_blocks, whole = lax.optimization_barrier((extended, inverse_blocks, whole))
    parts = [lax.slice_in_dim(whole, s * per, (s + 1) * per, axis=0) for s in range(streams)]
    picked = jnp.take(extended, margin, axis=0)
    local = jnp.einsum("jerb,jebc->jrc", picked, inverse_blocks, preferred_element_type=jnp.float32)
    for step in range(1, nb):
        parts = [halve(x, 1 + orders[s][step], *bits[orders[s][step]], jnp.float32) for s, x in enumerate(parts)]
        if step == 1:
            local, parts = lax.optimization_barrier((local, parts))
    mine = jnp.concatenate(parts, axis=0).reshape(total_blocks, inner, width)
    coarse_in = mine.astype(jnp.bfloat16)
    chosen = jnp.take(coarse_in, pattern_all, axis=0)
    solved = jnp.einsum(
        "nerc,necd->nrd", chosen, inverse_all, preferred_element_type=jnp.float32
    ).astype(jnp.bfloat16)
    solved = solved.reshape((total_blocks,) + (1,) * nb + (inner, width))
    outs = [lax.slice_in_dim(solved, s * per, (s + 1) * per, axis=0) for s in range(streams)]
    for step in reversed(range(1, nb)):
        outs = [double(y, 1 + orders[s][step], *bits[orders[s][step]]) for s, y in enumerate(outs)]
    own = jnp.concatenate(outs, axis=0).reshape(total_blocks, rhs // 2, width)
    got = lax.ppermute(own, bits[0][0], pairs(*bits[0]))
    own_rows = jnp.take(own, interface, axis=0)
    got_rows = jnp.take(got, interface, axis=0)
    lifted = jnp.where(
        own_half == 0,
        jnp.concatenate([own_rows, got_rows], axis=2),
        jnp.concatenate([got_rows, own_rows], axis=2),
    )

    spread = jnp.einsum("jqrc,jqbc->jrb", lifted, basis, preferred_element_type=jnp.float32)
    return (local + spread).astype(jnp.bfloat16)


def solution(mesh):
    in_specs = (
        P(("sub", "coarse"), None, None),
        P(("sub", "coarse"), None),
        P(("sub", "coarse"), None, None, None),
        P(("sub", "coarse"), None),
        P(("sub", "coarse"), None, None, None),
        P("coarse", None),
        P("coarse", None, None, None),
    )
    out_specs = P(("sub", "coarse"), None, None)
    return jax.shard_map(
        per_device, mesh=mesh, in_specs=in_specs, out_specs=out_specs, check_vma=False
    )
```

```python
import functools

import jax
import jax.numpy as jnp
from jax import lax
from jax.experimental import pallas as pl
from jax.experimental.pallas import tpu as pltpu
from jax.sharding import PartitionSpec as P


def restrict_kernel(links, half, residual_ref, basis_ref, out_ref, *, upper):
    j = pl.program_id(0)
    pairs_per = basis_ref.shape[1]
    rows = out_ref.shape[1]

    @pl.when(j == 0)
    def _():
        out_ref[...] = jnp.zeros_like(out_ref)

    for q in range(pairs_per):
        n = links[j * pairs_per + q]

        @pl.when(half[0] == upper)
        def _():
            out_ref[n] += jnp.dot(residual_ref[0, :rows], basis_ref[0, q], preferred_element_type=jnp.float32)

        @pl.when(half[0] != upper)
        def _():
            out_ref[n] += jnp.dot(residual_ref[0, rows:], basis_ref[0, q], preferred_element_type=jnp.float32)


def restrict(residual, basis, links, total_blocks, half, upper):
    count, rhs, size = residual.shape
    width = basis.shape[-1]
    rows = rhs // 2
    return pl.pallas_call(
        functools.partial(restrict_kernel, upper=upper),
        out_shape=jax.ShapeDtypeStruct((total_blocks, rows, width), jnp.float32),
        grid_spec=pltpu.PrefetchScalarGridSpec(
            num_scalar_prefetch=2,
            grid=(count,),
            in_specs=[
                pl.BlockSpec((1, rhs, size), lambda j, links, half: (j, 0, 0)),
                pl.BlockSpec((1, basis.shape[1], size, width), lambda j, links, half: (j, 0, 0, 0)),
            ],
            out_specs=pl.BlockSpec((total_blocks, rows, width), lambda j, links, half: (0, 0, 0)),
        ),
        compiler_params=pltpu.CompilerParams(dimension_semantics=("arbitrary",)),
        cost_estimate=pl.CostEstimate(
            flops=count * basis.shape[1] * rhs * size * width,
            bytes_accessed=residual.size * 2 + basis.size * 2 + total_blocks * rows * width * 4,
            transcendentals=0,
        ),
    )(links, half, residual, basis)


def with_halo(cells, sides, width):
    for axis, dim in sides:
        count = lax.axis_size(axis)
        ends = count - 1
        head = lax.slice_in_dim(cells, 0, width, axis=dim)
        tail = lax.slice_in_dim(cells, cells.shape[dim] - width, cells.shape[dim], axis=dim)
        cells = jnp.concatenate(
            [
                lax.ppermute(tail, axis, [(i, (i + 1) % count) for i in range(ends)]),
                cells,
                lax.ppermute(head, axis, [((i + 1) % count, i) for i in range(ends)]),
            ],
            axis=dim,
        )
    return cells


def device_bits():
    bits = []
    for axis in ("coarse", "sub"):
        size = lax.axis_size(axis)
        mask = 1
        while mask < size:
            bits.append((axis, mask))
            mask *= 2
        assert mask == size
    return bits


def bit_of(axis, mask):
    return (lax.axis_index(axis) // mask) % 2


def pairs(axis, mask):
    return [(i, i ^ mask) for i in range(lax.axis_size(axis))]


def halve(x, dim, axis, mask, wire):
    v = bit_of(axis, mask)
    keep = lax.dynamic_index_in_dim(x, v, axis=dim, keepdims=True)
    send = lax.dynamic_index_in_dim(x, 1 - v, axis=dim, keepdims=True)
    return keep + lax.ppermute(send.astype(wire), axis, pairs(axis, mask)).astype(x.dtype)


def double(y, dim, axis, mask):
    v = bit_of(axis, mask)
    recv = lax.ppermute(y, axis, pairs(axis, mask))
    return jnp.where(v == 0, jnp.concatenate([y, recv], axis=dim), jnp.concatenate([recv, y], axis=dim))


def stream_orders(nbits, streams):
    rest = list(range(1, nbits))
    orders = []
    for s in range(streams):
        k = (s * len(rest)) // streams
        orders.append([0] + rest[k:] + rest[:k])
    return orders


def per_device(residual, margin, inverse_blocks, interface, basis, coarse_pattern, coarse_inverse):
    rows, cols = coarse_inverse.shape[-2:]
    tags = jnp.broadcast_to(coarse_pattern.astype(jnp.bfloat16)[:, :, None, None], coarse_pattern.shape + (8, cols))
    packed = jnp.concatenate([coarse_inverse, tags], axis=2)
    xors = [0]
    for axis, mask in reversed([bit for bit in device_bits() if bit[0] == "coarse"]):
        packed = jnp.concatenate([packed, lax.ppermute(packed, axis, pairs(axis, mask))], axis=0)
        xors = xors + [x ^ mask for x in xors]
    slot_of = jnp.array([xors.index(x) for x in range(len(xors))], jnp.int32)
    own_rows = coarse_inverse.shape[0]
    labels = jnp.arange(len(xors) * own_rows, dtype=jnp.int32)
    order = slot_of[(labels // own_rows) ^ lax.axis_index("coarse")] * own_rows + labels % own_rows
    inverse_all = packed[:, :, :rows, :]
    pattern_all = packed[:, :, rows, 0].astype(jnp.int32)
    extended = with_halo(residual, ((("sub", "coarse"), 0),), 1)
    rhs = residual.shape[1]
    width = basis.shape[-1]
    total_blocks = pattern_all.shape[0]
    bits = device_bits()
    own_half = bit_of(*bits[0])
    links = interface.reshape(-1)
    half = own_half.reshape(1).astype(jnp.int32)
    send = restrict(residual, basis, links, total_blocks, half, 1)

    nb = len(bits)
    inner = rhs >> nb
    assert inner << nb == rhs
    streams = 3 if total_blocks % 3 == 0 else 1
    per = total_blocks // streams
    orders = stream_orders(nb, streams)
    got = lax.ppermute(send, bits[0][0], pairs(*bits[0]))
    whole = restrict(residual, basis, links, total_blocks, half, 0) + got
    whole = whole.reshape((total_blocks, 1) + (2,) * (nb - 1) + (inner, width))
    extended, inverse_blocks, whole = lax.optimization_barrier((extended, inverse_blocks, whole))
    parts = [lax.slice_in_dim(whole, s * per, (s + 1) * per, axis=0) for s in range(streams)]
    picked = jnp.take(extended, margin, axis=0)
    local = jnp.einsum("jerb,jebc->jrc", picked, inverse_blocks, preferred_element_type=jnp.float32)
    for step in range(1, nb):
        parts = [halve(x, 1 + orders[s][step], *bits[orders[s][step]], jnp.float32) for s, x in enumerate(parts)]
        if step == 1:
            local, parts = lax.optimization_barrier((local, parts))
    mine = jnp.concatenate(parts, axis=0).reshape(total_blocks, inner, width)
    coarse_in = mine.astype(jnp.bfloat16)
    chosen = jnp.take(coarse_in, pattern_all, axis=0)
    solved = jnp.einsum(
        "nerc,necd->nrd", chosen, inverse_all, preferred_element_type=jnp.float32
    ).astype(jnp.bfloat16)
    solved = jnp.take(solved, order, axis=0)
    solved = solved.reshape((total_blocks,) + (1,) * nb + (inner, width))
    outs = [lax.slice_in_dim(solved, s * per, (s + 1) * per, axis=0) for s in range(streams)]
    for step in reversed(range(1, nb)):
        outs = [double(y, 1 + orders[s][step], *bits[orders[s][step]]) for s, y in enumerate(outs)]
    own = jnp.concatenate(outs, axis=0).reshape(total_blocks, rhs // 2, width)
    got = lax.ppermute(own, bits[0][0], pairs(*bits[0]))
    own_rows = jnp.take(own, interface, axis=0)
    got_rows = jnp.take(got, interface, axis=0)
    lifted = jnp.where(
        own_half == 0,
        jnp.concatenate([own_rows, got_rows], axis=2),
        jnp.concatenate([got_rows, own_rows], axis=2),
    )

    spread = jnp.einsum("jqrc,jqbc->jrb", lifted, basis, preferred_element_type=jnp.float32)
    return (local + spread).astype(jnp.bfloat16)


def solution(mesh):
    in_specs = (
        P(("sub", "coarse"), None, None),
        P(("sub", "coarse"), None),
        P(("sub", "coarse"), None, None, None),
        P(("sub", "coarse"), None),
        P(("sub", "coarse"), None, None, None),
        P("coarse", None),
        P("coarse", None, None, None),
    )
    out_specs = P(("sub", "coarse"), None, None)
    return jax.shard_map(
        per_device, mesh=mesh, in_specs=in_specs, out_specs=out_specs, check_vma=False
    )
```

```python
import functools

import jax
import jax.numpy as jnp
from jax import lax
from jax.experimental import pallas as pl
from jax.experimental.pallas import tpu as pltpu
from jax.sharding import PartitionSpec as P


def restrict_kernel(links, half, residual_ref, basis_ref, out_ref, *, upper):
    j = pl.program_id(0)
    pairs_per = basis_ref.shape[1]
    rows = out_ref.shape[1]

    @pl.when(j == 0)
    def _():
        out_ref[...] = jnp.zeros_like(out_ref)

    for q in range(pairs_per):
        n = links[j * pairs_per + q]

        @pl.when(half[0] == upper)
        def _():
            out_ref[n] += jnp.dot(residual_ref[0, :rows], basis_ref[0, q], preferred_element_type=jnp.float32)

        @pl.when(half[0] != upper)
        def _():
            out_ref[n] += jnp.dot(residual_ref[0, rows:], basis_ref[0, q], preferred_element_type=jnp.float32)


def restrict(residual, basis, links, total_blocks, half, upper):
    count, rhs, size = residual.shape
    width = basis.shape[-1]
    rows = rhs // 2
    return pl.pallas_call(
        functools.partial(restrict_kernel, upper=upper),
        out_shape=jax.ShapeDtypeStruct((total_blocks, rows, width), jnp.float32),
        grid_spec=pltpu.PrefetchScalarGridSpec(
            num_scalar_prefetch=2,
            grid=(count,),
            in_specs=[
                pl.BlockSpec((1, rhs, size), lambda j, links, half: (j, 0, 0)),
                pl.BlockSpec((1, basis.shape[1], size, width), lambda j, links, half: (j, 0, 0, 0)),
            ],
            out_specs=pl.BlockSpec((total_blocks, rows, width), lambda j, links, half: (0, 0, 0)),
        ),
        compiler_params=pltpu.CompilerParams(dimension_semantics=("arbitrary",)),
        cost_estimate=pl.CostEstimate(
            flops=count * basis.shape[1] * rhs * size * width,
            bytes_accessed=residual.size * 2 + basis.size * 2 + total_blocks * rows * width * 4,
            transcendentals=0,
        ),
    )(links, half, residual, basis)


def with_halo(cells, sides, width):
    for axis, dim in sides:
        count = lax.axis_size(axis)
        ends = count - 1
        head = lax.slice_in_dim(cells, 0, width, axis=dim)
        tail = lax.slice_in_dim(cells, cells.shape[dim] - width, cells.shape[dim], axis=dim)
        cells = jnp.concatenate(
            [
                lax.ppermute(tail, axis, [(i, (i + 1) % count) for i in range(ends)]),
                cells,
                lax.ppermute(head, axis, [((i + 1) % count, i) for i in range(ends)]),
            ],
            axis=dim,
        )
    return cells


def device_bits():
    bits = []
    for axis in ("coarse", "sub"):
        size = lax.axis_size(axis)
        mask = 1
        while mask < size:
            bits.append((axis, mask))
            mask *= 2
        assert mask == size
    return bits


def bit_of(axis, mask):
    return (lax.axis_index(axis) // mask) % 2


def pairs(axis, mask):
    return [(i, i ^ mask) for i in range(lax.axis_size(axis))]


def halve(x, dim, axis, mask, wire):
    v = bit_of(axis, mask)
    keep = lax.dynamic_index_in_dim(x, v, axis=dim, keepdims=True)
    send = lax.dynamic_index_in_dim(x, 1 - v, axis=dim, keepdims=True)
    return keep + lax.ppermute(send.astype(wire), axis, pairs(axis, mask)).astype(x.dtype)


def double(y, dim, axis, mask):
    v = bit_of(axis, mask)
    recv = lax.ppermute(y, axis, pairs(axis, mask))
    return jnp.where(v == 0, jnp.concatenate([y, recv], axis=dim), jnp.concatenate([recv, y], axis=dim))


def stream_orders(nbits, streams):
    rest = list(range(1, nbits))
    orders = []
    for s in range(streams):
        k = (s * len(rest)) // streams
        orders.append([0] + rest[k:] + rest[:k])
    return orders


def per_device(residual, margin, inverse_blocks, interface, basis, coarse_pattern, coarse_inverse):
    rows, cols = coarse_inverse.shape[-2:]
    tags = jnp.broadcast_to(coarse_pattern.astype(jnp.bfloat16)[:, :, None, None], coarse_pattern.shape + (8, cols))
    packed = jnp.concatenate([coarse_inverse, tags], axis=2)
    own_rows = coarse_inverse.shape[0]
    extended = with_halo(residual, ((("sub", "coarse"), 0),), 1)
    rhs = residual.shape[1]
    width = basis.shape[-1]
    total_blocks = own_rows * lax.axis_size("coarse")
    bits = device_bits()
    own_half = bit_of(*bits[0])
    links = interface.reshape(-1)
    half = own_half.reshape(1).astype(jnp.int32)
    send = restrict(residual, basis, links, total_blocks, half, 1)

    nb = len(bits)
    inner = rhs >> nb
    assert inner << nb == rhs
    streams = 3 if total_blocks % 3 == 0 else 1
    per = total_blocks // streams
    orders = stream_orders(nb, streams)
    got = lax.ppermute(send, bits[0][0], pairs(*bits[0]))
    whole = restrict(residual, basis, links, total_blocks, half, 0) + got
    whole = whole.reshape((total_blocks, 1) + (2,) * (nb - 1) + (inner, width))
    extended, inverse_blocks, whole = lax.optimization_barrier((extended, inverse_blocks, whole))
    parts = [lax.slice_in_dim(whole, s * per, (s + 1) * per, axis=0) for s in range(streams)]
    picked = jnp.take(extended, margin, axis=0)
    local = jnp.einsum("jerb,jebc->jrc", picked, inverse_blocks, preferred_element_type=jnp.float32)
    exchanges = list(reversed([bit for bit in bits if bit[0] == "coarse"]))
    assert nb >= len(exchanges) + 2
    xors = [0]
    arriving = None
    for step in range(1, nb):
        parts = [halve(x, 1 + orders[s][step], *bits[orders[s][step]], jnp.float32) for s, x in enumerate(parts)]
        if step == 1:
            local, parts = lax.optimization_barrier((local, parts))
        k = step - 1
        if arriving is not None:
            arriving, parts = lax.optimization_barrier((arriving, parts))
            packed = jnp.concatenate([packed, arriving], axis=0)
            arriving = None
        if k < len(exchanges):
            packed, parts = lax.optimization_barrier((packed, parts))
            axis, mask = exchanges[k]
            arriving = lax.ppermute(packed, axis, pairs(axis, mask))
            xors = xors + [x ^ mask for x in xors]
    assert arriving is None
    slot_of = jnp.array([xors.index(x) for x in range(len(xors))], jnp.int32)
    labels = jnp.arange(len(xors) * own_rows, dtype=jnp.int32)
    order = slot_of[(labels // own_rows) ^ lax.axis_index("coarse")] * own_rows + labels % own_rows
    inverse_all = packed[:, :, :rows, :]
    pattern_all = packed[:, :, rows, 0].astype(jnp.int32)
    mine = jnp.concatenate(parts, axis=0).reshape(total_blocks, inner, width)
    coarse_in = mine.astype(jnp.bfloat16)
    chosen = jnp.take(coarse_in, pattern_all, axis=0)
    solved = jnp.einsum(
        "nerc,necd->nrd", chosen, inverse_all, preferred_element_type=jnp.float32
    ).astype(jnp.bfloat16)
    solved = jnp.take(solved, order, axis=0)
    solved = solved.reshape((total_blocks,) + (1,) * nb + (inner, width))
    outs = [lax.slice_in_dim(solved, s * per, (s + 1) * per, axis=0) for s in range(streams)]
    for step in reversed(range(1, nb)):
        outs = [double(y, 1 + orders[s][step], *bits[orders[s][step]]) for s, y in enumerate(outs)]
    own = jnp.concatenate(outs, axis=0).reshape(total_blocks, rhs // 2, width)
    got = lax.ppermute(own, bits[0][0], pairs(*bits[0]))
    own_rows = jnp.take(own, interface, axis=0)
    got_rows = jnp.take(got, interface, axis=0)
    lifted = jnp.where(
        own_half == 0,
        jnp.concatenate([own_rows, got_rows], axis=2),
        jnp.concatenate([got_rows, own_rows], axis=2),
    )

    spread = jnp.einsum("jqrc,jqbc->jrb", lifted, basis, preferred_element_type=jnp.float32)
    return (local + spread).astype(jnp.bfloat16)


def solution(mesh):
    in_specs = (
        P(("sub", "coarse"), None, None),
        P(("sub", "coarse"), None),
        P(("sub", "coarse"), None, None, None),
        P(("sub", "coarse"), None),
        P(("sub", "coarse"), None, None, None),
        P("coarse", None),
        P("coarse", None, None, None),
    )
    out_specs = P(("sub", "coarse"), None, None)
    return jax.shard_map(
        per_device, mesh=mesh, in_specs=in_specs, out_specs=out_specs, check_vma=False
    )
```

```python
import functools

import jax
import jax.numpy as jnp
from jax import lax
from jax.experimental import pallas as pl
from jax.experimental.pallas import tpu as pltpu
from jax.sharding import PartitionSpec as P


def restrict_kernel(links, half, residual_ref, basis_ref, out_ref, *, upper):
    j = pl.program_id(0)
    pairs_per = basis_ref.shape[1]
    rows = out_ref.shape[1]

    @pl.when(j == 0)
    def _():
        out_ref[...] = jnp.zeros_like(out_ref)

    for q in range(pairs_per):
        n = links[j * pairs_per + q]

        @pl.when(half[0] == upper)
        def _():
            out_ref[n] += jnp.dot(residual_ref[0, :rows], basis_ref[0, q], preferred_element_type=jnp.float32)

        @pl.when(half[0] != upper)
        def _():
            out_ref[n] += jnp.dot(residual_ref[0, rows:], basis_ref[0, q], preferred_element_type=jnp.float32)


def restrict(residual, basis, links, total_blocks, half, upper):
    count, rhs, size = residual.shape
    width = basis.shape[-1]
    rows = rhs // 2
    return pl.pallas_call(
        functools.partial(restrict_kernel, upper=upper),
        out_shape=jax.ShapeDtypeStruct((total_blocks, rows, width), jnp.float32),
        grid_spec=pltpu.PrefetchScalarGridSpec(
            num_scalar_prefetch=2,
            grid=(count,),
            in_specs=[
                pl.BlockSpec((1, rhs, size), lambda j, links, half: (j, 0, 0)),
                pl.BlockSpec((1, basis.shape[1], size, width), lambda j, links, half: (j, 0, 0, 0)),
            ],
            out_specs=pl.BlockSpec((total_blocks, rows, width), lambda j, links, half: (0, 0, 0)),
        ),
        compiler_params=pltpu.CompilerParams(dimension_semantics=("arbitrary",)),
        cost_estimate=pl.CostEstimate(
            flops=count * basis.shape[1] * rhs * size * width,
            bytes_accessed=residual.size * 2 + basis.size * 2 + total_blocks * rows * width * 4,
            transcendentals=0,
        ),
    )(links, half, residual, basis)


def with_halo(cells, sides, width):
    for axis, dim in sides:
        count = lax.axis_size(axis)
        ends = count - 1
        head = lax.slice_in_dim(cells, 0, width, axis=dim)
        tail = lax.slice_in_dim(cells, cells.shape[dim] - width, cells.shape[dim], axis=dim)
        cells = jnp.concatenate(
            [
                lax.ppermute(tail, axis, [(i, (i + 1) % count) for i in range(ends)]),
                cells,
                lax.ppermute(head, axis, [((i + 1) % count, i) for i in range(ends)]),
            ],
            axis=dim,
        )
    return cells


def device_bits():
    bits = []
    for axis in ("coarse", "sub"):
        size = lax.axis_size(axis)
        mask = 1
        while mask < size:
            bits.append((axis, mask))
            mask *= 2
        assert mask == size
    return bits


def bit_of(axis, mask):
    return (lax.axis_index(axis) // mask) % 2


def pairs(axis, mask):
    return [(i, i ^ mask) for i in range(lax.axis_size(axis))]


def halve(x, dim, axis, mask, wire):
    v = bit_of(axis, mask)
    keep = lax.dynamic_index_in_dim(x, v, axis=dim, keepdims=True)
    send = lax.dynamic_index_in_dim(x, 1 - v, axis=dim, keepdims=True)
    return keep + lax.ppermute(send.astype(wire), axis, pairs(axis, mask)).astype(x.dtype)


def double(y, dim, axis, mask):
    v = bit_of(axis, mask)
    recv = lax.ppermute(y, axis, pairs(axis, mask))
    return jnp.where(v == 0, jnp.concatenate([y, recv], axis=dim), jnp.concatenate([recv, y], axis=dim))


def stream_orders(nbits, streams):
    rest = list(range(1, nbits))
    orders = []
    for s in range(streams):
        k = (s * len(rest)) // streams
        orders.append([0] + rest[k:] + rest[:k])
    return orders


def per_device(residual, margin, inverse_blocks, interface, basis, coarse_pattern, coarse_inverse):
    rows, cols = coarse_inverse.shape[-2:]
    tags = jnp.broadcast_to(coarse_pattern.astype(jnp.bfloat16)[:, :, None, None], coarse_pattern.shape + (8, cols))
    packed = jnp.concatenate([coarse_inverse, tags], axis=2)
    own_rows = coarse_inverse.shape[0]
    extended = with_halo(residual, ((("sub", "coarse"), 0),), 1)
    rhs = residual.shape[1]
    width = basis.shape[-1]
    total_blocks = own_rows * lax.axis_size("coarse")
    bits = device_bits()
    own_half = bit_of(*bits[0])
    links = interface.reshape(-1)
    half = own_half.reshape(1).astype(jnp.int32)
    send = restrict(residual, basis, links, total_blocks, half, 1)

    nb = len(bits)
    inner = rhs >> nb
    assert inner << nb == rhs
    streams = 3 if total_blocks % 3 == 0 else 1
    per = total_blocks // streams
    orders = stream_orders(nb, streams)
    got = lax.ppermute(send, bits[0][0], pairs(*bits[0]))
    whole = restrict(residual, basis, links, total_blocks, half, 0) + got
    whole = whole.reshape((total_blocks, 1) + (2,) * (nb - 1) + (inner, width))
    exchanges = list(reversed([bit for bit in bits if bit[0] == "coarse"]))
    assert nb >= len(exchanges) + 1
    arriving = lax.ppermute(packed, exchanges[0][0], pairs(*exchanges[0]))
    xors = [0, exchanges[0][1]]
    extended, inverse_blocks, whole, arriving = lax.optimization_barrier((extended, inverse_blocks, whole, arriving))
    packed = jnp.concatenate([packed, arriving], axis=0)
    arriving = None
    parts = [lax.slice_in_dim(whole, s * per, (s + 1) * per, axis=0) for s in range(streams)]
    picked = jnp.take(extended, margin, axis=0)
    local = jnp.einsum("jerb,jebc->jrc", picked, inverse_blocks, preferred_element_type=jnp.float32)
    for step in range(1, nb):
        parts = [halve(x, 1 + orders[s][step], *bits[orders[s][step]], jnp.float32) for s, x in enumerate(parts)]
        if step == 1:
            local, parts = lax.optimization_barrier((local, parts))
        k = step
        if arriving is not None:
            arriving, parts = lax.optimization_barrier((arriving, parts))
            packed = jnp.concatenate([packed, arriving], axis=0)
            arriving = None
        if k < len(exchanges):
            packed, parts = lax.optimization_barrier((packed, parts))
            axis, mask = exchanges[k]
            arriving = lax.ppermute(packed, axis, pairs(axis, mask))
            xors = xors + [x ^ mask for x in xors]
    assert arriving is None
    slot_of = jnp.array([xors.index(x) for x in range(len(xors))], jnp.int32)
    labels = jnp.arange(len(xors) * own_rows, dtype=jnp.int32)
    order = slot_of[(labels // own_rows) ^ lax.axis_index("coarse")] * own_rows + labels % own_rows
    inverse_all = packed[:, :, :rows, :]
    pattern_all = packed[:, :, rows, 0].astype(jnp.int32)
    mine = jnp.concatenate(parts, axis=0).reshape(total_blocks, inner, width)
    coarse_in = mine.astype(jnp.bfloat16)
    chosen = jnp.take(coarse_in, pattern_all, axis=0)
    solved = jnp.einsum(
        "nerc,necd->nrd", chosen, inverse_all, preferred_element_type=jnp.float32
    ).astype(jnp.bfloat16)
    solved = jnp.take(solved, order, axis=0)
    solved = solved.reshape((total_blocks,) + (1,) * nb + (inner, width))
    outs = [lax.slice_in_dim(solved, s * per, (s + 1) * per, axis=0) for s in range(streams)]
    for step in reversed(range(1, nb)):
        outs = [double(y, 1 + orders[s][step], *bits[orders[s][step]]) for s, y in enumerate(outs)]
    own = jnp.concatenate(outs, axis=0).reshape(total_blocks, rhs // 2, width)
    got = lax.ppermute(own, bits[0][0], pairs(*bits[0]))
    own_rows = jnp.take(own, interface, axis=0)
    got_rows = jnp.take(got, interface, axis=0)
    lifted = jnp.where(
        own_half == 0,
        jnp.concatenate([own_rows, got_rows], axis=2),
        jnp.concatenate([got_rows, own_rows], axis=2),
    )

    spread = jnp.einsum("jqrc,jqbc->jrb", lifted, basis, preferred_element_type=jnp.float32)
    return (local + spread).astype(jnp.bfloat16)


def solution(mesh):
    in_specs = (
        P(("sub", "coarse"), None, None),
        P(("sub", "coarse"), None),
        P(("sub", "coarse"), None, None, None),
        P(("sub", "coarse"), None),
        P(("sub", "coarse"), None, None, None),
        P("coarse", None),
        P("coarse", None, None, None),
    )
    out_specs = P(("sub", "coarse"), None, None)
    return jax.shard_map(
        per_device, mesh=mesh, in_specs=in_specs, out_specs=out_specs, check_vma=False
    )
```

```python
import functools

import jax
import jax.numpy as jnp
from jax import lax
from jax.experimental import pallas as pl
from jax.experimental.pallas import tpu as pltpu
from jax.sharding import PartitionSpec as P


def restrict_kernel(links, half, residual_ref, basis_ref, out_ref, *, upper):
    j = pl.program_id(0)
    pairs_per = basis_ref.shape[1]
    rows = out_ref.shape[1]

    @pl.when(j == 0)
    def _():
        out_ref[...] = jnp.zeros_like(out_ref)

    for q in range(pairs_per):
        n = links[j * pairs_per + q]

        @pl.when(half[0] == upper)
        def _():
            out_ref[n] += jnp.dot(residual_ref[0, :rows], basis_ref[0, q], preferred_element_type=jnp.float32)

        @pl.when(half[0] != upper)
        def _():
            out_ref[n] += jnp.dot(residual_ref[0, rows:], basis_ref[0, q], preferred_element_type=jnp.float32)


def restrict(residual, basis, links, total_blocks, half, upper):
    count, rhs, size = residual.shape
    width = basis.shape[-1]
    rows = rhs // 2
    return pl.pallas_call(
        functools.partial(restrict_kernel, upper=upper),
        out_shape=jax.ShapeDtypeStruct((total_blocks, rows, width), jnp.float32),
        grid_spec=pltpu.PrefetchScalarGridSpec(
            num_scalar_prefetch=2,
            grid=(count,),
            in_specs=[
                pl.BlockSpec((1, rhs, size), lambda j, links, half: (j, 0, 0)),
                pl.BlockSpec((1, basis.shape[1], size, width), lambda j, links, half: (j, 0, 0, 0)),
            ],
            out_specs=pl.BlockSpec((total_blocks, rows, width), lambda j, links, half: (0, 0, 0)),
        ),
        compiler_params=pltpu.CompilerParams(dimension_semantics=("arbitrary",)),
        cost_estimate=pl.CostEstimate(
            flops=count * basis.shape[1] * rhs * size * width,
            bytes_accessed=residual.size * 2 + basis.size * 2 + total_blocks * rows * width * 4,
            transcendentals=0,
        ),
    )(links, half, residual, basis)


def with_halo(cells, sides, width):
    for axis, dim in sides:
        count = lax.axis_size(axis)
        ends = count - 1
        head = lax.slice_in_dim(cells, 0, width, axis=dim)
        tail = lax.slice_in_dim(cells, cells.shape[dim] - width, cells.shape[dim], axis=dim)
        cells = jnp.concatenate(
            [
                lax.ppermute(tail, axis, [(i, (i + 1) % count) for i in range(ends)]),
                cells,
                lax.ppermute(head, axis, [((i + 1) % count, i) for i in range(ends)]),
            ],
            axis=dim,
        )
    return cells


def device_bits():
    bits = []
    for axis in ("coarse", "sub"):
        size = lax.axis_size(axis)
        mask = 1
        while mask < size:
            bits.append((axis, mask))
            mask *= 2
        assert mask == size
    return bits


def bit_of(axis, mask):
    return (lax.axis_index(axis) // mask) % 2


def pairs(axis, mask):
    return [(i, i ^ mask) for i in range(lax.axis_size(axis))]


def halve(x, dim, axis, mask, wire):
    v = bit_of(axis, mask)
    keep = lax.dynamic_index_in_dim(x, v, axis=dim, keepdims=True)
    send = lax.dynamic_index_in_dim(x, 1 - v, axis=dim, keepdims=True)
    return keep + lax.ppermute(send.astype(wire), axis, pairs(axis, mask)).astype(x.dtype)


def double(y, dim, axis, mask):
    v = bit_of(axis, mask)
    recv = lax.ppermute(y, axis, pairs(axis, mask))
    return jnp.where(v == 0, jnp.concatenate([y, recv], axis=dim), jnp.concatenate([recv, y], axis=dim))


def stream_orders(nbits, streams):
    rest = list(range(1, nbits))
    orders = []
    for s in range(streams):
        k = (s * len(rest)) // streams
        orders.append([0] + rest[k:] + rest[:k])
    return orders


def per_device(residual, margin, inverse_blocks, interface, basis, coarse_pattern, coarse_inverse):
    rows, cols = coarse_inverse.shape[-2:]
    tags = jnp.broadcast_to(coarse_pattern.astype(jnp.bfloat16)[:, :, None, None], coarse_pattern.shape + (8, cols))
    packed = jnp.concatenate([coarse_inverse, tags], axis=2)
    own_rows = coarse_inverse.shape[0]
    extended = with_halo(residual, ((("sub", "coarse"), 0),), 1)
    rhs = residual.shape[1]
    width = basis.shape[-1]
    total_blocks = own_rows * lax.axis_size("coarse")
    bits = device_bits()
    own_half = bit_of(*bits[0])
    exchanges = list(reversed([bit for bit in bits if bit[0] == "coarse"]))
    assert len(bits) >= len(exchanges) + 1
    arriving = lax.ppermute(packed, exchanges[0][0], pairs(*exchanges[0]))
    xors = [0, exchanges[0][1]]
    residual, extended, arriving = lax.optimization_barrier((residual, extended, arriving))
    packed = jnp.concatenate([packed, arriving], axis=0)
    arriving = None
    links = interface.reshape(-1)
    half = own_half.reshape(1).astype(jnp.int32)
    send = restrict(residual, basis, links, total_blocks, half, 1)

    nb = len(bits)
    inner = rhs >> nb
    assert inner << nb == rhs
    streams = 3 if total_blocks % 3 == 0 else 1
    per = total_blocks // streams
    orders = stream_orders(nb, streams)
    got = lax.ppermute(send, bits[0][0], pairs(*bits[0]))
    whole = restrict(residual, basis, links, total_blocks, half, 0) + got
    whole = whole.reshape((total_blocks, 1) + (2,) * (nb - 1) + (inner, width))
    extended, inverse_blocks, whole = lax.optimization_barrier((extended, inverse_blocks, whole))
    parts = [lax.slice_in_dim(whole, s * per, (s + 1) * per, axis=0) for s in range(streams)]
    picked = jnp.take(extended, margin, axis=0)
    local = jnp.einsum("jerb,jebc->jrc", picked, inverse_blocks, preferred_element_type=jnp.float32)
    for step in range(1, nb):
        parts = [halve(x, 1 + orders[s][step], *bits[orders[s][step]], jnp.float32) for s, x in enumerate(parts)]
        if step == 1:
            local, parts = lax.optimization_barrier((local, parts))
        k = step
        if arriving is not None:
            arriving, parts = lax.optimization_barrier((arriving, parts))
            packed = jnp.concatenate([packed, arriving], axis=0)
            arriving = None
        if k < len(exchanges):
            packed, parts = lax.optimization_barrier((packed, parts))
            axis, mask = exchanges[k]
            arriving = lax.ppermute(packed, axis, pairs(axis, mask))
            xors = xors + [x ^ mask for x in xors]
    assert arriving is None
    slot_of = jnp.array([xors.index(x) for x in range(len(xors))], jnp.int32)
    labels = jnp.arange(len(xors) * own_rows, dtype=jnp.int32)
    order = slot_of[(labels // own_rows) ^ lax.axis_index("coarse")] * own_rows + labels % own_rows
    inverse_all = packed[:, :, :rows, :]
    pattern_all = packed[:, :, rows, 0].astype(jnp.int32)
    mine = jnp.concatenate(parts, axis=0).reshape(total_blocks, inner, width)
    coarse_in = mine.astype(jnp.bfloat16)
    chosen = jnp.take(coarse_in, pattern_all, axis=0)
    solved = jnp.einsum(
        "nerc,necd->nrd", chosen, inverse_all, preferred_element_type=jnp.float32
    ).astype(jnp.bfloat16)
    solved = jnp.take(solved, order, axis=0)
    solved = solved.reshape((total_blocks,) + (1,) * nb + (inner, width))
    outs = [lax.slice_in_dim(solved, s * per, (s + 1) * per, axis=0) for s in range(streams)]
    for step in reversed(range(1, nb)):
        outs = [double(y, 1 + orders[s][step], *bits[orders[s][step]]) for s, y in enumerate(outs)]
    own = jnp.concatenate(outs, axis=0).reshape(total_blocks, rhs // 2, width)
    got = lax.ppermute(own, bits[0][0], pairs(*bits[0]))
    own_rows = jnp.take(own, interface, axis=0)
    got_rows = jnp.take(got, interface, axis=0)
    lifted = jnp.where(
        own_half == 0,
        jnp.concatenate([own_rows, got_rows], axis=2),
        jnp.concatenate([got_rows, own_rows], axis=2),
    )

    spread = jnp.einsum("jqrc,jqbc->jrb", lifted, basis, preferred_element_type=jnp.float32)
    return (local + spread).astype(jnp.bfloat16)


def solution(mesh):
    in_specs = (
        P(("sub", "coarse"), None, None),
        P(("sub", "coarse"), None),
        P(("sub", "coarse"), None, None, None),
        P(("sub", "coarse"), None),
        P(("sub", "coarse"), None, None, None),
        P("coarse", None),
        P("coarse", None, None, None),
    )
    out_specs = P(("sub", "coarse"), None, None)
    return jax.shard_map(
        per_device, mesh=mesh, in_specs=in_specs, out_specs=out_specs, check_vma=False
    )
```

```python
import functools

import jax
import jax.numpy as jnp
from jax import lax
from jax.experimental import pallas as pl
from jax.experimental.pallas import tpu as pltpu
from jax.sharding import PartitionSpec as P


def restrict_kernel(links, half, residual_ref, basis_ref, out_ref, *, upper):
    j = pl.program_id(0)
    pairs_per = basis_ref.shape[1]
    rows = out_ref.shape[1]

    @pl.when(j == 0)
    def _():
        out_ref[...] = jnp.zeros_like(out_ref)

    for q in range(pairs_per):
        n = links[j * pairs_per + q]

        @pl.when(half[0] == upper)
        def _():
            out_ref[n] += jnp.dot(residual_ref[0, :rows], basis_ref[0, q], preferred_element_type=jnp.float32)

        @pl.when(half[0] != upper)
        def _():
            out_ref[n] += jnp.dot(residual_ref[0, rows:], basis_ref[0, q], preferred_element_type=jnp.float32)


def restrict(residual, basis, links, total_blocks, half, upper):
    count, rhs, size = residual.shape
    width = basis.shape[-1]
    rows = rhs // 2
    return pl.pallas_call(
        functools.partial(restrict_kernel, upper=upper),
        out_shape=jax.ShapeDtypeStruct((total_blocks, rows, width), jnp.float32),
        grid_spec=pltpu.PrefetchScalarGridSpec(
            num_scalar_prefetch=2,
            grid=(count,),
            in_specs=[
                pl.BlockSpec((1, rhs, size), lambda j, links, half: (j, 0, 0)),
                pl.BlockSpec((1, basis.shape[1], size, width), lambda j, links, half: (j, 0, 0, 0)),
            ],
            out_specs=pl.BlockSpec((total_blocks, rows, width), lambda j, links, half: (0, 0, 0)),
        ),
        compiler_params=pltpu.CompilerParams(dimension_semantics=("arbitrary",)),
        cost_estimate=pl.CostEstimate(
            flops=count * basis.shape[1] * rhs * size * width,
            bytes_accessed=residual.size * 2 + basis.size * 2 + total_blocks * rows * width * 4,
            transcendentals=0,
        ),
    )(links, half, residual, basis)


def with_halo(cells, sides, width):
    for axis, dim in sides:
        count = lax.axis_size(axis)
        ends = count - 1
        head = lax.slice_in_dim(cells, 0, width, axis=dim)
        tail = lax.slice_in_dim(cells, cells.shape[dim] - width, cells.shape[dim], axis=dim)
        cells = jnp.concatenate(
            [
                lax.ppermute(tail, axis, [(i, (i + 1) % count) for i in range(ends)]),
                cells,
                lax.ppermute(head, axis, [((i + 1) % count, i) for i in range(ends)]),
            ],
            axis=dim,
        )
    return cells


def device_bits():
    bits = []
    for axis in ("coarse", "sub"):
        size = lax.axis_size(axis)
        mask = 1
        while mask < size:
            bits.append((axis, mask))
            mask *= 2
        assert mask == size
    return bits


def bit_of(axis, mask):
    return (lax.axis_index(axis) // mask) % 2


def pairs(axis, mask):
    return [(i, i ^ mask) for i in range(lax.axis_size(axis))]


def halve(x, dim, axis, mask, wire):
    v = bit_of(axis, mask)
    keep = lax.dynamic_index_in_dim(x, v, axis=dim, keepdims=True)
    send = lax.dynamic_index_in_dim(x, 1 - v, axis=dim, keepdims=True)
    return keep + lax.ppermute(send.astype(wire), axis, pairs(axis, mask)).astype(x.dtype)


def double(y, dim, axis, mask):
    v = bit_of(axis, mask)
    recv = lax.ppermute(y, axis, pairs(axis, mask))
    return jnp.where(v == 0, jnp.concatenate([y, recv], axis=dim), jnp.concatenate([recv, y], axis=dim))


def stream_orders(nbits, streams):
    rest = list(range(1, nbits))
    orders = []
    for s in range(streams):
        k = (s * len(rest)) // streams
        orders.append([0] + rest[k:] + rest[:k])
    return orders


def per_device(residual, margin, inverse_blocks, interface, basis, coarse_pattern, coarse_inverse):
    rows, cols = coarse_inverse.shape[-2:]
    tags = jnp.broadcast_to(coarse_pattern.astype(jnp.bfloat16)[:, :, None, None], coarse_pattern.shape + (8, cols))
    packed = jnp.concatenate([coarse_inverse, tags], axis=2)
    own_rows = coarse_inverse.shape[0]
    extended = with_halo(residual, ((("sub", "coarse"), 0),), 1)
    rhs = residual.shape[1]
    width = basis.shape[-1]
    total_blocks = own_rows * lax.axis_size("coarse")
    bits = device_bits()
    own_half = bit_of(*bits[0])
    links = interface.reshape(-1)
    half = own_half.reshape(1).astype(jnp.int32)
    send = restrict(residual, basis, links, total_blocks, half, 1)

    nb = len(bits)
    inner = rhs >> nb
    assert inner << nb == rhs
    streams = 3 if total_blocks % 3 == 0 else 1
    per = total_blocks // streams
    orders = stream_orders(nb, streams)
    got = lax.ppermute(send, bits[0][0], pairs(*bits[0]))
    whole = restrict(residual, basis, links, total_blocks, half, 0) + got
    whole = whole.reshape((total_blocks, 1) + (2,) * (nb - 1) + (inner, width))
    exchanges = list(reversed([bit for bit in bits if bit[0] == "coarse"]))
    assert nb >= len(exchanges) + 1
    arriving = lax.ppermute(packed, exchanges[0][0], pairs(*exchanges[0]))
    xors = [0, exchanges[0][1]]
    extended, inverse_blocks, whole, arriving = lax.optimization_barrier((extended, inverse_blocks, whole, arriving))
    packed = jnp.concatenate([packed, arriving], axis=0)
    arriving = None
    parts = [lax.slice_in_dim(whole, s * per, (s + 1) * per, axis=0) for s in range(streams)]
    picked = jnp.take(extended, margin, axis=0)
    local = jnp.einsum("jerb,jebc->jrc", picked, inverse_blocks, preferred_element_type=jnp.float32)
    for step in range(1, nb):
        parts = [halve(x, 1 + orders[s][step], *bits[orders[s][step]], jnp.float32) for s, x in enumerate(parts)]
        if step == 1:
            local, parts = lax.optimization_barrier((local, parts))
        k = step
        if arriving is not None:
            arriving, parts = lax.optimization_barrier((arriving, parts))
            packed = jnp.concatenate([packed, arriving], axis=0)
            arriving = None
        if k < len(exchanges):
            packed, parts = lax.optimization_barrier((packed, parts))
            axis, mask = exchanges[k]
            arriving = lax.ppermute(packed, axis, pairs(axis, mask))
            xors = xors + [x ^ mask for x in xors]
    assert arriving is None
    slot_of = jnp.array([xors.index(x) for x in range(len(xors))], jnp.int32)
    labels = jnp.arange(len(xors) * own_rows, dtype=jnp.int32)
    order = slot_of[(labels // own_rows) ^ lax.axis_index("coarse")] * own_rows + labels % own_rows
    inverse_all = packed[:, :, :rows, :]
    pattern_all = packed[:, :, rows, 0].astype(jnp.int32)
    mine = jnp.concatenate(parts, axis=0).reshape(total_blocks, inner, width)
    coarse_in = mine.astype(jnp.bfloat16)
    chosen = jnp.take(coarse_in, pattern_all, axis=0)
    solved = jnp.einsum(
        "nerc,necd->nrd", chosen, inverse_all, preferred_element_type=jnp.float32
    ).astype(jnp.bfloat16)
    solved = jnp.take(solved, order, axis=0)
    solved = solved.reshape((total_blocks,) + (1,) * nb + (inner, width))
    for step in reversed(range(1, nb)):
        solved = double(solved, 1 + orders[0][step], *bits[orders[0][step]])
    own = solved.reshape(total_blocks, rhs // 2, width)
    got = lax.ppermute(own, bits[0][0], pairs(*bits[0]))
    own_rows = jnp.take(own, interface, axis=0)
    got_rows = jnp.take(got, interface, axis=0)
    lifted = jnp.where(
        own_half == 0,
        jnp.concatenate([own_rows, got_rows], axis=2),
        jnp.concatenate([got_rows, own_rows], axis=2),
    )

    spread = jnp.einsum("jqrc,jqbc->jrb", lifted, basis, preferred_element_type=jnp.float32)
    return (local + spread).astype(jnp.bfloat16)


def solution(mesh):
    in_specs = (
        P(("sub", "coarse"), None, None),
        P(("sub", "coarse"), None),
        P(("sub", "coarse"), None, None, None),
        P(("sub", "coarse"), None),
        P(("sub", "coarse"), None, None, None),
        P("coarse", None),
        P("coarse", None, None, None),
    )
    out_specs = P(("sub", "coarse"), None, None)
    return jax.shard_map(
        per_device, mesh=mesh, in_specs=in_specs, out_specs=out_specs, check_vma=False
    )
```

```python
import functools

import jax
import jax.numpy as jnp
from jax import lax
from jax.experimental import pallas as pl
from jax.experimental.pallas import tpu as pltpu
from jax.sharding import PartitionSpec as P


def restrict_kernel(links, half, residual_ref, basis_ref, out_ref, *, upper):
    j = pl.program_id(0)
    pairs_per = basis_ref.shape[1]
    rows = out_ref.shape[1]

    @pl.when(j == 0)
    def _():
        out_ref[...] = jnp.zeros_like(out_ref)

    for q in range(pairs_per):
        n = links[j * pairs_per + q]

        @pl.when(half[0] == upper)
        def _():
            out_ref[n] += jnp.dot(residual_ref[0, :rows], basis_ref[0, q], preferred_element_type=jnp.float32)

        @pl.when(half[0] != upper)
        def _():
            out_ref[n] += jnp.dot(residual_ref[0, rows:], basis_ref[0, q], preferred_element_type=jnp.float32)


def restrict(residual, basis, links, total_blocks, half, upper):
    count, rhs, size = residual.shape
    width = basis.shape[-1]
    rows = rhs // 2
    return pl.pallas_call(
        functools.partial(restrict_kernel, upper=upper),
        out_shape=jax.ShapeDtypeStruct((total_blocks, rows, width), jnp.float32),
        grid_spec=pltpu.PrefetchScalarGridSpec(
            num_scalar_prefetch=2,
            grid=(count,),
            in_specs=[
                pl.BlockSpec((1, rhs, size), lambda j, links, half: (j, 0, 0)),
                pl.BlockSpec((1, basis.shape[1], size, width), lambda j, links, half: (j, 0, 0, 0)),
            ],
            out_specs=pl.BlockSpec((total_blocks, rows, width), lambda j, links, half: (0, 0, 0)),
        ),
        compiler_params=pltpu.CompilerParams(dimension_semantics=("arbitrary",)),
        cost_estimate=pl.CostEstimate(
            flops=count * basis.shape[1] * rhs * size * width,
            bytes_accessed=residual.size * 2 + basis.size * 2 + total_blocks * rows * width * 4,
            transcendentals=0,
        ),
    )(links, half, residual, basis)


def with_halo(cells, sides, width):
    for axis, dim in sides:
        count = lax.axis_size(axis)
        ends = count - 1
        head = lax.slice_in_dim(cells, 0, width, axis=dim)
        tail = lax.slice_in_dim(cells, cells.shape[dim] - width, cells.shape[dim], axis=dim)
        cells = jnp.concatenate(
            [
                lax.ppermute(tail, axis, [(i, (i + 1) % count) for i in range(ends)]),
                cells,
                lax.ppermute(head, axis, [((i + 1) % count, i) for i in range(ends)]),
            ],
            axis=dim,
        )
    return cells


def device_bits():
    bits = []
    for axis in ("coarse", "sub"):
        size = lax.axis_size(axis)
        mask = 1
        while mask < size:
            bits.append((axis, mask))
            mask *= 2
        assert mask == size
    return bits


def bit_of(axis, mask):
    return (lax.axis_index(axis) // mask) % 2


def pairs(axis, mask):
    return [(i, i ^ mask) for i in range(lax.axis_size(axis))]


def halve(x, dim, axis, mask, wire):
    v = bit_of(axis, mask)
    keep = lax.dynamic_index_in_dim(x, v, axis=dim, keepdims=True)
    send = lax.dynamic_index_in_dim(x, 1 - v, axis=dim, keepdims=True)
    return keep + lax.ppermute(send.astype(wire), axis, pairs(axis, mask)).astype(x.dtype)


def double(y, dim, axis, mask):
    v = bit_of(axis, mask)
    recv = lax.ppermute(y, axis, pairs(axis, mask))
    return jnp.where(v == 0, jnp.concatenate([y, recv], axis=dim), jnp.concatenate([recv, y], axis=dim))


def stream_orders(nbits, streams):
    rest = list(range(1, nbits))
    orders = []
    for s in range(streams):
        k = (s * len(rest)) // streams
        orders.append([0] + rest[k:] + rest[:k])
    return orders


def per_device(residual, margin, inverse_blocks, interface, basis, coarse_pattern, coarse_inverse):
    rows, cols = coarse_inverse.shape[-2:]
    tags = jnp.broadcast_to(coarse_pattern.astype(jnp.bfloat16)[:, :, None, None], coarse_pattern.shape + (8, cols))
    packed = jnp.concatenate([coarse_inverse, tags], axis=2)
    own_rows = coarse_inverse.shape[0]
    extended = with_halo(residual, ((("sub", "coarse"), 0),), 1)
    rhs = residual.shape[1]
    width = basis.shape[-1]
    total_blocks = own_rows * lax.axis_size("coarse")
    bits = device_bits()
    own_half = bit_of(*bits[0])
    links = interface.reshape(-1)
    half = own_half.reshape(1).astype(jnp.int32)
    send = restrict(residual, basis, links, total_blocks, half, 1)

    nb = len(bits)
    inner = rhs >> nb
    assert inner << nb == rhs
    streams = 3 if total_blocks % 3 == 0 else 1
    per = total_blocks // streams
    orders = stream_orders(nb, streams)
    got = lax.ppermute(send, bits[0][0], pairs(*bits[0]))
    whole = restrict(residual, basis, links, total_blocks, half, 0) + got
    whole = whole.reshape((total_blocks, 1) + (2,) * (nb - 1) + (inner, width))
    exchanges = list(reversed([bit for bit in bits if bit[0] == "coarse"]))
    assert nb >= len(exchanges) + 1
    arriving = lax.ppermute(packed, exchanges[0][0], pairs(*exchanges[0]))
    xors = [0, exchanges[0][1]]
    margin, inverse_blocks, whole, arriving = lax.optimization_barrier((margin, inverse_blocks, whole, arriving))
    packed = jnp.concatenate([packed, arriving], axis=0)
    arriving = None
    parts = [lax.slice_in_dim(whole, s * per, (s + 1) * per, axis=0) for s in range(streams)]
    picked = jnp.take(extended, margin, axis=0)
    local = jnp.einsum("jerb,jebc->jrc", picked, inverse_blocks, preferred_element_type=jnp.float32)
    for step in range(1, nb):
        parts = [halve(x, 1 + orders[s][step], *bits[orders[s][step]], jnp.float32) for s, x in enumerate(parts)]
        if step == 1:
            local, parts = lax.optimization_barrier((local, parts))
        k = step
        if arriving is not None:
            arriving, parts = lax.optimization_barrier((arriving, parts))
            packed = jnp.concatenate([packed, arriving], axis=0)
            arriving = None
        if k < len(exchanges):
            packed, parts = lax.optimization_barrier((packed, parts))
            axis, mask = exchanges[k]
            arriving = lax.ppermute(packed, axis, pairs(axis, mask))
            xors = xors + [x ^ mask for x in xors]
    assert arriving is None
    slot_of = jnp.array([xors.index(x) for x in range(len(xors))], jnp.int32)
    labels = jnp.arange(len(xors) * own_rows, dtype=jnp.int32)
    order = slot_of[(labels // own_rows) ^ lax.axis_index("coarse")] * own_rows + labels % own_rows
    inverse_all = packed[:, :, :rows, :]
    pattern_all = packed[:, :, rows, 0].astype(jnp.int32)
    mine = jnp.concatenate(parts, axis=0).reshape(total_blocks, inner, width)
    coarse_in = mine.astype(jnp.bfloat16)
    chosen = jnp.take(coarse_in, pattern_all, axis=0)
    solved = jnp.einsum(
        "nerc,necd->nrd", chosen, inverse_all, preferred_element_type=jnp.float32
    ).astype(jnp.bfloat16)
    solved = jnp.take(solved, order, axis=0)
    solved = solved.reshape((total_blocks,) + (1,) * nb + (inner, width))
    outs = [lax.slice_in_dim(solved, s * per, (s + 1) * per, axis=0) for s in range(streams)]
    for step in reversed(range(1, nb)):
        outs = [double(y, 1 + orders[s][step], *bits[orders[s][step]]) for s, y in enumerate(outs)]
    own = jnp.concatenate(outs, axis=0).reshape(total_blocks, rhs // 2, width)
    got = lax.ppermute(own, bits[0][0], pairs(*bits[0]))
    own_rows = jnp.take(own, interface, axis=0)
    got_rows = jnp.take(got, interface, axis=0)
    lifted = jnp.where(
        own_half == 0,
        jnp.concatenate([own_rows, got_rows], axis=2),
        jnp.concatenate([got_rows, own_rows], axis=2),
    )

    spread = jnp.einsum("jqrc,jqbc->jrb", lifted, basis, preferred_element_type=jnp.float32)
    return (local + spread).astype(jnp.bfloat16)


def solution(mesh):
    in_specs = (
        P(("sub", "coarse"), None, None),
        P(("sub", "coarse"), None),
        P(("sub", "coarse"), None, None, None),
        P(("sub", "coarse"), None),
        P(("sub", "coarse"), None, None, None),
        P("coarse", None),
        P("coarse", None, None, None),
    )
    out_specs = P(("sub", "coarse"), None, None)
    return jax.shard_map(
        per_device, mesh=mesh, in_specs=in_specs, out_specs=out_specs, check_vma=False
    )
```

```python
import functools

import jax
import jax.numpy as jnp
from jax import lax
from jax.experimental import pallas as pl
from jax.experimental.pallas import tpu as pltpu
from jax.sharding import PartitionSpec as P


def restrict_kernel(links, half, residual_ref, basis_ref, out_ref, *, upper):
    j = pl.program_id(0)
    pairs_per = basis_ref.shape[1]
    rows = out_ref.shape[1]

    @pl.when(j == 0)
    def _():
        out_ref[...] = jnp.zeros_like(out_ref)

    for q in range(pairs_per):
        n = links[j * pairs_per + q]

        @pl.when(half[0] == upper)
        def _():
            out_ref[n] += jnp.dot(residual_ref[0, :rows], basis_ref[0, q], preferred_element_type=jnp.float32)

        @pl.when(half[0] != upper)
        def _():
            out_ref[n] += jnp.dot(residual_ref[0, rows:], basis_ref[0, q], preferred_element_type=jnp.float32)


def restrict(residual, basis, links, total_blocks, half, upper):
    count, rhs, size = residual.shape
    width = basis.shape[-1]
    rows = rhs // 2
    return pl.pallas_call(
        functools.partial(restrict_kernel, upper=upper),
        out_shape=jax.ShapeDtypeStruct((total_blocks, rows, width), jnp.float32),
        grid_spec=pltpu.PrefetchScalarGridSpec(
            num_scalar_prefetch=2,
            grid=(count,),
            in_specs=[
                pl.BlockSpec((1, rhs, size), lambda j, links, half: (j, 0, 0)),
                pl.BlockSpec((1, basis.shape[1], size, width), lambda j, links, half: (j, 0, 0, 0)),
            ],
            out_specs=pl.BlockSpec((total_blocks, rows, width), lambda j, links, half: (0, 0, 0)),
        ),
        compiler_params=pltpu.CompilerParams(dimension_semantics=("arbitrary",)),
        cost_estimate=pl.CostEstimate(
            flops=count * basis.shape[1] * rhs * size * width,
            bytes_accessed=residual.size * 2 + basis.size * 2 + total_blocks * rows * width * 4,
            transcendentals=0,
        ),
    )(links, half, residual, basis)


def with_halo(cells, sides, width):
    for axis, dim in sides:
        count = lax.axis_size(axis)
        ends = count - 1
        head = lax.slice_in_dim(cells, 0, width, axis=dim)
        tail = lax.slice_in_dim(cells, cells.shape[dim] - width, cells.shape[dim], axis=dim)
        cells = jnp.concatenate(
            [
                lax.ppermute(tail, axis, [(i, (i + 1) % count) for i in range(ends)]),
                cells,
                lax.ppermute(head, axis, [((i + 1) % count, i) for i in range(ends)]),
            ],
            axis=dim,
        )
    return cells


def device_bits():
    bits = []
    for axis in ("coarse", "sub"):
        size = lax.axis_size(axis)
        mask = 1
        while mask < size:
            bits.append((axis, mask))
            mask *= 2
        assert mask == size
    return bits


def bit_of(axis, mask):
    return (lax.axis_index(axis) // mask) % 2


def pairs(axis, mask):
    return [(i, i ^ mask) for i in range(lax.axis_size(axis))]


def halve(x, dim, axis, mask, wire):
    v = bit_of(axis, mask)
    keep = lax.dynamic_index_in_dim(x, v, axis=dim, keepdims=True)
    send = lax.dynamic_index_in_dim(x, 1 - v, axis=dim, keepdims=True)
    return keep + lax.ppermute(send.astype(wire), axis, pairs(axis, mask)).astype(x.dtype)


def double(y, dim, axis, mask):
    v = bit_of(axis, mask)
    recv = lax.ppermute(y, axis, pairs(axis, mask))
    return jnp.where(v == 0, jnp.concatenate([y, recv], axis=dim), jnp.concatenate([recv, y], axis=dim))


def stream_orders(nbits, streams):
    rest = list(range(1, nbits))
    orders = []
    for s in range(streams):
        k = (s * len(rest)) // streams
        orders.append([0] + rest[k:] + rest[:k])
    return orders


def per_device(residual, margin, inverse_blocks, interface, basis, coarse_pattern, coarse_inverse):
    rows, cols = coarse_inverse.shape[-2:]
    tags = jnp.broadcast_to(coarse_pattern.astype(jnp.bfloat16)[:, :, None, None], coarse_pattern.shape + (8, cols))
    packed = jnp.concatenate([coarse_inverse, tags], axis=2)
    own_rows = coarse_inverse.shape[0]
    extended = with_halo(residual, ((("sub", "coarse"), 0),), 1)
    rhs = residual.shape[1]
    width = basis.shape[-1]
    total_blocks = own_rows * lax.axis_size("coarse")
    bits = device_bits()
    own_half = bit_of(*bits[0])
    links = interface.reshape(-1)
    half = own_half.reshape(1).astype(jnp.int32)
    send = restrict(residual, basis, links, total_blocks, half, 1)

    nb = len(bits)
    inner = rhs >> nb
    assert inner << nb == rhs
    streams = 3 if total_blocks % 3 == 0 else 1
    per = total_blocks // streams
    orders = stream_orders(nb, streams)
    got = lax.ppermute(send, bits[0][0], pairs(*bits[0]))
    whole = restrict(residual, basis, links, total_blocks, half, 0) + got
    whole = whole.reshape((total_blocks, 1) + (2,) * (nb - 1) + (inner, width))
    exchanges = list(reversed([bit for bit in bits if bit[0] == "coarse"]))
    assert nb >= len(exchanges) + 1
    arriving = lax.ppermute(packed, exchanges[0][0], pairs(*exchanges[0]))
    xors = [0, exchanges[0][1]]
    extended, inverse_blocks, whole, arriving = lax.optimization_barrier((extended, inverse_blocks, whole, arriving))
    packed = jnp.concatenate([packed, arriving], axis=0)
    arriving = None
    parts = [lax.slice_in_dim(whole, s * per, (s + 1) * per, axis=0) for s in range(streams)]
    split_at = margin.shape[0] // 2
    picked = jnp.take(extended, margin[:split_at], axis=0)
    local = [jnp.einsum("jerb,jebc->jrc", picked, inverse_blocks[:split_at], preferred_element_type=jnp.float32)]
    for step in range(1, nb):
        parts = [halve(x, 1 + orders[s][step], *bits[orders[s][step]], jnp.float32) for s, x in enumerate(parts)]
        if step == 1:
            local[0], extended, parts = lax.optimization_barrier((local[0], extended, parts))
            picked = jnp.take(extended, margin[split_at:], axis=0)
            local.append(jnp.einsum("jerb,jebc->jrc", picked, inverse_blocks[split_at:], preferred_element_type=jnp.float32))
        if step == 2:
            local[1], parts = lax.optimization_barrier((local[1], parts))
        k = step
        if arriving is not None:
            arriving, parts = lax.optimization_barrier((arriving, parts))
            packed = jnp.concatenate([packed, arriving], axis=0)
            arriving = None
        if k < len(exchanges):
            packed, parts = lax.optimization_barrier((packed, parts))
            axis, mask = exchanges[k]
            arriving = lax.ppermute(packed, axis, pairs(axis, mask))
            xors = xors + [x ^ mask for x in xors]
    assert arriving is None
    slot_of = jnp.array([xors.index(x) for x in range(len(xors))], jnp.int32)
    labels = jnp.arange(len(xors) * own_rows, dtype=jnp.int32)
    order = slot_of[(labels // own_rows) ^ lax.axis_index("coarse")] * own_rows + labels % own_rows
    inverse_all = packed[:, :, :rows, :]
    pattern_all = packed[:, :, rows, 0].astype(jnp.int32)
    mine = jnp.concatenate(parts, axis=0).reshape(total_blocks, inner, width)
    coarse_in = mine.astype(jnp.bfloat16)
    chosen = jnp.take(coarse_in, pattern_all, axis=0)
    solved = jnp.einsum(
        "nerc,necd->nrd", chosen, inverse_all, preferred_element_type=jnp.float32
    ).astype(jnp.bfloat16)
    solved = jnp.take(solved, order, axis=0)
    solved = solved.reshape((total_blocks,) + (1,) * nb + (inner, width))
    outs = [lax.slice_in_dim(solved, s * per, (s + 1) * per, axis=0) for s in range(streams)]
    for step in reversed(range(1, nb)):
        outs = [double(y, 1 + orders[s][step], *bits[orders[s][step]]) for s, y in enumerate(outs)]
    own = jnp.concatenate(outs, axis=0).reshape(total_blocks, rhs // 2, width)
    got = lax.ppermute(own, bits[0][0], pairs(*bits[0]))
    own_rows = jnp.take(own, interface, axis=0)
    got_rows = jnp.take(got, interface, axis=0)
    lifted = jnp.where(
        own_half == 0,
        jnp.concatenate([own_rows, got_rows], axis=2),
        jnp.concatenate([got_rows, own_rows], axis=2),
    )

    spread = jnp.einsum("jqrc,jqbc->jrb", lifted, basis, preferred_element_type=jnp.float32)
    return (jnp.concatenate(local, axis=0) + spread).astype(jnp.bfloat16)


def solution(mesh):
    in_specs = (
        P(("sub", "coarse"), None, None),
        P(("sub", "coarse"), None),
        P(("sub", "coarse"), None, None, None),
        P(("sub", "coarse"), None),
        P(("sub", "coarse"), None, None, None),
        P("coarse", None),
        P("coarse", None, None, None),
    )
    out_specs = P(("sub", "coarse"), None, None)
    return jax.shard_map(
        per_device, mesh=mesh, in_specs=in_specs, out_specs=out_specs, check_vma=False
    )
```

```python
import functools

import jax
import jax.numpy as jnp
from jax import lax
from jax.experimental import pallas as pl
from jax.experimental.pallas import tpu as pltpu
from jax.sharding import PartitionSpec as P


def restrict_kernel(links, half, residual_ref, basis_ref, out_ref, *, upper):
    j = pl.program_id(0)
    pairs_per = basis_ref.shape[1]
    rows = out_ref.shape[1]

    @pl.when(j == 0)
    def _():
        out_ref[...] = jnp.zeros_like(out_ref)

    for q in range(pairs_per):
        n = links[j * pairs_per + q]

        @pl.when(half[0] == upper)
        def _():
            out_ref[n] += jnp.dot(residual_ref[0, :rows], basis_ref[0, q], preferred_element_type=jnp.float32)

        @pl.when(half[0] != upper)
        def _():
            out_ref[n] += jnp.dot(residual_ref[0, rows:], basis_ref[0, q], preferred_element_type=jnp.float32)


def restrict(residual, basis, links, total_blocks, half, upper):
    count, rhs, size = residual.shape
    width = basis.shape[-1]
    rows = rhs // 2
    return pl.pallas_call(
        functools.partial(restrict_kernel, upper=upper),
        out_shape=jax.ShapeDtypeStruct((total_blocks, rows, width), jnp.float32),
        grid_spec=pltpu.PrefetchScalarGridSpec(
            num_scalar_prefetch=2,
            grid=(count,),
            in_specs=[
                pl.BlockSpec((1, rhs, size), lambda j, links, half: (j, 0, 0)),
                pl.BlockSpec((1, basis.shape[1], size, width), lambda j, links, half: (j, 0, 0, 0)),
            ],
            out_specs=pl.BlockSpec((total_blocks, rows, width), lambda j, links, half: (0, 0, 0)),
        ),
        compiler_params=pltpu.CompilerParams(dimension_semantics=("arbitrary",)),
        cost_estimate=pl.CostEstimate(
            flops=count * basis.shape[1] * rhs * size * width,
            bytes_accessed=residual.size * 2 + basis.size * 2 + total_blocks * rows * width * 4,
            transcendentals=0,
        ),
    )(links, half, residual, basis)


def with_halo(cells, sides, width):
    for axis, dim in sides:
        count = lax.axis_size(axis)
        ends = count - 1
        head = lax.slice_in_dim(cells, 0, width, axis=dim)
        tail = lax.slice_in_dim(cells, cells.shape[dim] - width, cells.shape[dim], axis=dim)
        cells = jnp.concatenate(
            [
                lax.ppermute(tail, axis, [(i, (i + 1) % count) for i in range(ends)]),
                cells,
                lax.ppermute(head, axis, [((i + 1) % count, i) for i in range(ends)]),
            ],
            axis=dim,
        )
    return cells


def device_bits():
    bits = []
    for axis in ("coarse", "sub"):
        size = lax.axis_size(axis)
        mask = 1
        while mask < size:
            bits.append((axis, mask))
            mask *= 2
        assert mask == size
    return bits


def bit_of(axis, mask):
    return (lax.axis_index(axis) // mask) % 2


def pairs(axis, mask):
    return [(i, i ^ mask) for i in range(lax.axis_size(axis))]


def halve(x, dim, axis, mask, wire):
    v = bit_of(axis, mask)
    keep = lax.dynamic_index_in_dim(x, v, axis=dim, keepdims=True)
    send = lax.dynamic_index_in_dim(x, 1 - v, axis=dim, keepdims=True)
    return keep + lax.ppermute(send.astype(wire), axis, pairs(axis, mask)).astype(x.dtype)


def double(y, dim, axis, mask):
    v = bit_of(axis, mask)
    recv = lax.ppermute(y, axis, pairs(axis, mask))
    return jnp.where(v == 0, jnp.concatenate([y, recv], axis=dim), jnp.concatenate([recv, y], axis=dim))


def stream_orders(nbits, streams):
    rest = list(range(1, nbits))
    orders = []
    for s in range(streams):
        k = (s * len(rest)) // streams
        orders.append([0] + rest[k:] + rest[:k])
    return orders


def per_device(residual, margin, inverse_blocks, interface, basis, coarse_pattern, coarse_inverse):
    rows, cols = coarse_inverse.shape[-2:]
    tags = jnp.broadcast_to(coarse_pattern.astype(jnp.bfloat16)[:, :, None, None], coarse_pattern.shape + (8, cols))
    packed = jnp.concatenate([coarse_inverse, tags], axis=2)
    own_rows = coarse_inverse.shape[0]
    extended = with_halo(residual, ((("sub", "coarse"), 0),), 1)
    rhs = residual.shape[1]
    width = basis.shape[-1]
    total_blocks = own_rows * lax.axis_size("coarse")
    bits = device_bits()
    own_half = bit_of(*bits[0])
    links = interface.reshape(-1)
    half = own_half.reshape(1).astype(jnp.int32)
    send = restrict(residual, basis, links, total_blocks, half, 1)

    nb = len(bits)
    inner = rhs >> nb
    assert inner << nb == rhs
    streams = 3 if total_blocks % 3 == 0 else 1
    per = total_blocks // streams
    orders = stream_orders(nb, streams)
    got = lax.ppermute(send, bits[0][0], pairs(*bits[0]))
    whole = restrict(residual, basis, links, total_blocks, half, 0) + got
    whole = whole.reshape((total_blocks, 1) + (2,) * (nb - 1) + (inner, width))
    exchanges = list(reversed([bit for bit in bits if bit[0] == "coarse"]))
    assert nb >= len(exchanges) + 1
    arriving = lax.ppermute(packed, exchanges[0][0], pairs(*exchanges[0]))
    xors = [0, exchanges[0][1]]
    extended, inverse_blocks, whole, arriving = lax.optimization_barrier((extended, inverse_blocks, whole, arriving))
    packed = jnp.concatenate([packed, arriving], axis=0)
    arriving = None
    parts = [lax.slice_in_dim(whole, s * per, (s + 1) * per, axis=0) for s in range(streams)]
    count = margin.shape[0]
    sizes = [count // 2] + [1] * (count - count // 2)
    assert nb - 1 >= len(sizes)
    edges = [sum(sizes[:k]) for k in range(len(sizes) + 1)]

    def solve_blocks(k, extended):
        picked = jnp.take(extended, margin[edges[k]:edges[k + 1]], axis=0)
        return jnp.einsum(
            "jerb,jebc->jrc", picked, inverse_blocks[edges[k]:edges[k + 1]], preferred_element_type=jnp.float32
        )

    local = [solve_blocks(0, extended)]
    for step in range(1, nb):
        parts = [halve(x, 1 + orders[s][step], *bits[orders[s][step]], jnp.float32) for s, x in enumerate(parts)]
        if step <= len(sizes):
            local[step - 1], extended, parts = lax.optimization_barrier((local[step - 1], extended, parts))
            if step < len(sizes):
                local.append(solve_blocks(step, extended))
        k = step
        if arriving is not None:
            arriving, parts = lax.optimization_barrier((arriving, parts))
            packed = jnp.concatenate([packed, arriving], axis=0)
            arriving = None
        if k < len(exchanges):
            packed, parts = lax.optimization_barrier((packed, parts))
            axis, mask = exchanges[k]
            arriving = lax.ppermute(packed, axis, pairs(axis, mask))
            xors = xors + [x ^ mask for x in xors]
    assert arriving is None
    slot_of = jnp.array([xors.index(x) for x in range(len(xors))], jnp.int32)
    labels = jnp.arange(len(xors) * own_rows, dtype=jnp.int32)
    order = slot_of[(labels // own_rows) ^ lax.axis_index("coarse")] * own_rows + labels % own_rows
    inverse_all = packed[:, :, :rows, :]
    pattern_all = packed[:, :, rows, 0].astype(jnp.int32)
    mine = jnp.concatenate(parts, axis=0).reshape(total_blocks, inner, width)
    coarse_in = mine.astype(jnp.bfloat16)
    chosen = jnp.take(coarse_in, pattern_all, axis=0)
    solved = jnp.einsum(
        "nerc,necd->nrd", chosen, inverse_all, preferred_element_type=jnp.float32
    ).astype(jnp.bfloat16)
    solved = jnp.take(solved, order, axis=0)
    solved = solved.reshape((total_blocks,) + (1,) * nb + (inner, width))
    outs = [lax.slice_in_dim(solved, s * per, (s + 1) * per, axis=0) for s in range(streams)]
    for step in reversed(range(1, nb)):
        outs = [double(y, 1 + orders[s][step], *bits[orders[s][step]]) for s, y in enumerate(outs)]
    own = jnp.concatenate(outs, axis=0).reshape(total_blocks, rhs // 2, width)
    got = lax.ppermute(own, bits[0][0], pairs(*bits[0]))
    own_rows = jnp.take(own, interface, axis=0)
    got_rows = jnp.take(got, interface, axis=0)
    lifted = jnp.where(
        own_half == 0,
        jnp.concatenate([own_rows, got_rows], axis=2),
        jnp.concatenate([got_rows, own_rows], axis=2),
    )

    spread = jnp.einsum("jqrc,jqbc->jrb", lifted, basis, preferred_element_type=jnp.float32)
    return (jnp.concatenate(local, axis=0) + spread).astype(jnp.bfloat16)


def solution(mesh):
    in_specs = (
        P(("sub", "coarse"), None, None),
        P(("sub", "coarse"), None),
        P(("sub", "coarse"), None, None, None),
        P(("sub", "coarse"), None),
        P(("sub", "coarse"), None, None, None),
        P("coarse", None),
        P("coarse", None, None, None),
    )
    out_specs = P(("sub", "coarse"), None, None)
    return jax.shard_map(
        per_device, mesh=mesh, in_specs=in_specs, out_specs=out_specs, check_vma=False
    )
```

```python
import functools

import jax
import jax.numpy as jnp
from jax import lax
from jax.experimental import pallas as pl
from jax.experimental.pallas import tpu as pltpu
from jax.sharding import PartitionSpec as P


def restrict_kernel(links, half, residual_ref, basis_ref, out_ref, *, upper):
    j = pl.program_id(0)
    pairs_per = basis_ref.shape[1]
    rows = out_ref.shape[1]

    @pl.when(j == 0)
    def _():
        out_ref[...] = jnp.zeros_like(out_ref)

    for q in range(pairs_per):
        n = links[j * pairs_per + q]

        @pl.when(half[0] == upper)
        def _():
            out_ref[n] += jnp.dot(residual_ref[0, :rows], basis_ref[0, q], preferred_element_type=jnp.float32)

        @pl.when(half[0] != upper)
        def _():
            out_ref[n] += jnp.dot(residual_ref[0, rows:], basis_ref[0, q], preferred_element_type=jnp.float32)


def restrict(residual, basis, links, total_blocks, half, upper):
    count, rhs, size = residual.shape
    width = basis.shape[-1]
    rows = rhs // 2
    return pl.pallas_call(
        functools.partial(restrict_kernel, upper=upper),
        out_shape=jax.ShapeDtypeStruct((total_blocks, rows, width), jnp.float32),
        grid_spec=pltpu.PrefetchScalarGridSpec(
            num_scalar_prefetch=2,
            grid=(count,),
            in_specs=[
                pl.BlockSpec((1, rhs, size), lambda j, links, half: (j, 0, 0)),
                pl.BlockSpec((1, basis.shape[1], size, width), lambda j, links, half: (j, 0, 0, 0)),
            ],
            out_specs=pl.BlockSpec((total_blocks, rows, width), lambda j, links, half: (0, 0, 0)),
        ),
        compiler_params=pltpu.CompilerParams(dimension_semantics=("arbitrary",)),
        cost_estimate=pl.CostEstimate(
            flops=count * basis.shape[1] * rhs * size * width,
            bytes_accessed=residual.size * 2 + basis.size * 2 + total_blocks * rows * width * 4,
            transcendentals=0,
        ),
    )(links, half, residual, basis)


def with_halo(cells, sides, width):
    for axis, dim in sides:
        count = lax.axis_size(axis)
        ends = count - 1
        head = lax.slice_in_dim(cells, 0, width, axis=dim)
        tail = lax.slice_in_dim(cells, cells.shape[dim] - width, cells.shape[dim], axis=dim)
        cells = jnp.concatenate(
            [
                lax.ppermute(tail, axis, [(i, (i + 1) % count) for i in range(ends)]),
                cells,
                lax.ppermute(head, axis, [((i + 1) % count, i) for i in range(ends)]),
            ],
            axis=dim,
        )
    return cells


def device_bits():
    bits = []
    for axis in ("coarse", "sub"):
        size = lax.axis_size(axis)
        mask = 1
        while mask < size:
            bits.append((axis, mask))
            mask *= 2
        assert mask == size
    return bits


def bit_of(axis, mask):
    return (lax.axis_index(axis) // mask) % 2


def pairs(axis, mask):
    return [(i, i ^ mask) for i in range(lax.axis_size(axis))]


def halve(x, dim, axis, mask, wire):
    v = bit_of(axis, mask)
    keep = lax.dynamic_index_in_dim(x, v, axis=dim, keepdims=True)
    send = lax.dynamic_index_in_dim(x, 1 - v, axis=dim, keepdims=True)
    return keep + lax.ppermute(send.astype(wire), axis, pairs(axis, mask)).astype(x.dtype)


def double(y, dim, axis, mask):
    v = bit_of(axis, mask)
    recv = lax.ppermute(y, axis, pairs(axis, mask))
    return jnp.where(v == 0, jnp.concatenate([y, recv], axis=dim), jnp.concatenate([recv, y], axis=dim))


def stream_orders(nbits, streams):
    rest = list(range(1, nbits))
    orders = []
    for s in range(streams):
        k = (s * len(rest)) // streams
        orders.append([0] + rest[k:] + rest[:k])
    return orders


def per_device(residual, margin, inverse_blocks, interface, basis, coarse_pattern, coarse_inverse):
    rows, cols = coarse_inverse.shape[-2:]
    tags = jnp.broadcast_to(coarse_pattern.astype(jnp.bfloat16)[:, :, None, None], coarse_pattern.shape + (8, cols))
    packed = jnp.concatenate([coarse_inverse, tags], axis=2)
    own_rows = coarse_inverse.shape[0]
    extended = with_halo(residual, ((("sub", "coarse"), 0),), 1)
    rhs = residual.shape[1]
    width = basis.shape[-1]
    total_blocks = own_rows * lax.axis_size("coarse")
    bits = device_bits()
    own_half = bit_of(*bits[0])
    links = interface.reshape(-1)
    half = own_half.reshape(1).astype(jnp.int32)
    send = restrict(residual, basis, links, total_blocks, half, 1)

    nb = len(bits)
    inner = rhs >> nb
    assert inner << nb == rhs
    streams = 3 if total_blocks % 3 == 0 else 1
    per = total_blocks // streams
    orders = stream_orders(nb, streams)
    got = lax.ppermute(send, bits[0][0], pairs(*bits[0]))
    whole = restrict(residual, basis, links, total_blocks, half, 0) + got
    whole = whole.reshape((total_blocks, 1) + (2,) * (nb - 1) + (inner, width))
    exchanges = list(reversed([bit for bit in bits if bit[0] == "coarse"]))
    assert nb >= len(exchanges) + 1
    arriving = lax.ppermute(packed, exchanges[0][0], pairs(*exchanges[0]))
    xors = [0, exchanges[0][1]]
    extended, inverse_blocks, whole, arriving = lax.optimization_barrier((extended, inverse_blocks, whole, arriving))
    packed = jnp.concatenate([packed, arriving], axis=0)
    arriving = None
    parts = [lax.slice_in_dim(whole, s * per, (s + 1) * per, axis=0) for s in range(streams)]
    split_at = (3 * margin.shape[0]) // 4
    picked = jnp.take(extended, margin[:split_at], axis=0)
    local = [jnp.einsum("jerb,jebc->jrc", picked, inverse_blocks[:split_at], preferred_element_type=jnp.float32)]
    for step in range(1, nb):
        parts = [halve(x, 1 + orders[s][step], *bits[orders[s][step]], jnp.float32) for s, x in enumerate(parts)]
        if step == 1:
            local[0], extended, parts = lax.optimization_barrier((local[0], extended, parts))
            picked = jnp.take(extended, margin[split_at:], axis=0)
            local.append(jnp.einsum("jerb,jebc->jrc", picked, inverse_blocks[split_at:], preferred_element_type=jnp.float32))
        if step == 2:
            local[1], parts = lax.optimization_barrier((local[1], parts))
        k = step
        if arriving is not None:
            arriving, parts = lax.optimization_barrier((arriving, parts))
            packed = jnp.concatenate([packed, arriving], axis=0)
            arriving = None
        if k < len(exchanges):
            packed, parts = lax.optimization_barrier((packed, parts))
            axis, mask = exchanges[k]
            arriving = lax.ppermute(packed, axis, pairs(axis, mask))
            xors = xors + [x ^ mask for x in xors]
    assert arriving is None
    slot_of = jnp.array([xors.index(x) for x in range(len(xors))], jnp.int32)
    labels = jnp.arange(len(xors) * own_rows, dtype=jnp.int32)
    order = slot_of[(labels // own_rows) ^ lax.axis_index("coarse")] * own_rows + labels % own_rows
    inverse_all = packed[:, :, :rows, :]
    pattern_all = packed[:, :, rows, 0].astype(jnp.int32)
    mine = jnp.concatenate(parts, axis=0).reshape(total_blocks, inner, width)
    coarse_in = mine.astype(jnp.bfloat16)
    chosen = jnp.take(coarse_in, pattern_all, axis=0)
    solved = jnp.einsum(
        "nerc,necd->nrd", chosen, inverse_all, preferred_element_type=jnp.float32
    ).astype(jnp.bfloat16)
    solved = jnp.take(solved, order, axis=0)
    solved = solved.reshape((total_blocks,) + (1,) * nb + (inner, width))
    outs = [lax.slice_in_dim(solved, s * per, (s + 1) * per, axis=0) for s in range(streams)]
    for step in reversed(range(1, nb)):
        outs = [double(y, 1 + orders[s][step], *bits[orders[s][step]]) for s, y in enumerate(outs)]
    own = jnp.concatenate(outs, axis=0).reshape(total_blocks, rhs // 2, width)
    got = lax.ppermute(own, bits[0][0], pairs(*bits[0]))
    own_rows = jnp.take(own, interface, axis=0)
    got_rows = jnp.take(got, interface, axis=0)
    lifted = jnp.where(
        own_half == 0,
        jnp.concatenate([own_rows, got_rows], axis=2),
        jnp.concatenate([got_rows, own_rows], axis=2),
    )

    spread = jnp.einsum("jqrc,jqbc->jrb", lifted, basis, preferred_element_type=jnp.float32)
    return (jnp.concatenate(local, axis=0) + spread).astype(jnp.bfloat16)


def solution(mesh):
    in_specs = (
        P(("sub", "coarse"), None, None),
        P(("sub", "coarse"), None),
        P(("sub", "coarse"), None, None, None),
        P(("sub", "coarse"), None),
        P(("sub", "coarse"), None, None, None),
        P("coarse", None),
        P("coarse", None, None, None),
    )
    out_specs = P(("sub", "coarse"), None, None)
    return jax.shard_map(
        per_device, mesh=mesh, in_specs=in_specs, out_specs=out_specs, check_vma=False
    )
```

```python
import functools

import jax
import jax.numpy as jnp
from jax import lax
from jax.experimental import pallas as pl
from jax.experimental.pallas import tpu as pltpu
from jax.sharding import PartitionSpec as P


def restrict_kernel(links, half, residual_ref, basis_ref, out_ref, *, upper):
    j = pl.program_id(0)
    pairs_per = basis_ref.shape[1]
    rows = out_ref.shape[1]

    @pl.when(j == 0)
    def _():
        out_ref[...] = jnp.zeros_like(out_ref)

    for q in range(pairs_per):
        n = links[j * pairs_per + q]

        @pl.when(half[0] == upper)
        def _():
            out_ref[n] += jnp.dot(residual_ref[0, :rows], basis_ref[0, q], preferred_element_type=jnp.float32)

        @pl.when(half[0] != upper)
        def _():
            out_ref[n] += jnp.dot(residual_ref[0, rows:], basis_ref[0, q], preferred_element_type=jnp.float32)


def restrict(residual, basis, links, total_blocks, half, upper):
    count, rhs, size = residual.shape
    width = basis.shape[-1]
    rows = rhs // 2
    return pl.pallas_call(
        functools.partial(restrict_kernel, upper=upper),
        out_shape=jax.ShapeDtypeStruct((total_blocks, rows, width), jnp.float32),
        grid_spec=pltpu.PrefetchScalarGridSpec(
            num_scalar_prefetch=2,
            grid=(count,),
            in_specs=[
                pl.BlockSpec((1, rhs, size), lambda j, links, half: (j, 0, 0)),
                pl.BlockSpec((1, basis.shape[1], size, width), lambda j, links, half: (j, 0, 0, 0)),
            ],
            out_specs=pl.BlockSpec((total_blocks, rows, width), lambda j, links, half: (0, 0, 0)),
        ),
        compiler_params=pltpu.CompilerParams(dimension_semantics=("arbitrary",)),
        cost_estimate=pl.CostEstimate(
            flops=count * basis.shape[1] * rhs * size * width,
            bytes_accessed=residual.size * 2 + basis.size * 2 + total_blocks * rows * width * 4,
            transcendentals=0,
        ),
    )(links, half, residual, basis)


def with_halo(cells, sides, width):
    for axis, dim in sides:
        count = lax.axis_size(axis)
        ends = count - 1
        head = lax.slice_in_dim(cells, 0, width, axis=dim)
        tail = lax.slice_in_dim(cells, cells.shape[dim] - width, cells.shape[dim], axis=dim)
        cells = jnp.concatenate(
            [
                lax.ppermute(tail, axis, [(i, (i + 1) % count) for i in range(ends)]),
                cells,
                lax.ppermute(head, axis, [((i + 1) % count, i) for i in range(ends)]),
            ],
            axis=dim,
        )
    return cells


def device_bits():
    bits = []
    for axis in ("coarse", "sub"):
        size = lax.axis_size(axis)
        mask = 1
        while mask < size:
            bits.append((axis, mask))
            mask *= 2
        assert mask == size
    return bits


def bit_of(axis, mask):
    return (lax.axis_index(axis) // mask) % 2


def pairs(axis, mask):
    return [(i, i ^ mask) for i in range(lax.axis_size(axis))]


def halve(x, dim, axis, mask, wire):
    v = bit_of(axis, mask)
    keep = lax.dynamic_index_in_dim(x, v, axis=dim, keepdims=True)
    send = lax.dynamic_index_in_dim(x, 1 - v, axis=dim, keepdims=True)
    return keep + lax.ppermute(send.astype(wire), axis, pairs(axis, mask)).astype(x.dtype)


def double(y, dim, axis, mask):
    v = bit_of(axis, mask)
    recv = lax.ppermute(y, axis, pairs(axis, mask))
    return jnp.where(v == 0, jnp.concatenate([y, recv], axis=dim), jnp.concatenate([recv, y], axis=dim))


def stream_orders(nbits, streams):
    rest = list(range(1, nbits))
    orders = []
    for s in range(streams):
        k = (s * len(rest)) // streams
        orders.append([0] + rest[k:] + rest[:k])
    return orders


def per_device(residual, margin, inverse_blocks, interface, basis, coarse_pattern, coarse_inverse):
    rows, cols = coarse_inverse.shape[-2:]
    tags = jnp.broadcast_to(coarse_pattern.astype(jnp.bfloat16)[:, :, None, None], coarse_pattern.shape + (8, cols))
    packed = jnp.concatenate([coarse_inverse, tags], axis=2)
    own_rows = coarse_inverse.shape[0]
    extended = with_halo(residual, ((("sub", "coarse"), 0),), 1)
    rhs = residual.shape[1]
    width = basis.shape[-1]
    total_blocks = own_rows * lax.axis_size("coarse")
    bits = device_bits()
    own_half = bit_of(*bits[0])
    links = interface.reshape(-1)
    half = own_half.reshape(1).astype(jnp.int32)
    send = restrict(residual, basis, links, total_blocks, half, 1)

    nb = len(bits)
    inner = rhs >> nb
    assert inner << nb == rhs
    streams = 3 if total_blocks % 3 == 0 else 1
    per = total_blocks // streams
    orders = stream_orders(nb, streams)
    got = lax.ppermute(send, bits[0][0], pairs(*bits[0]))
    whole = restrict(residual, basis, links, total_blocks, half, 0) + got
    whole = whole.reshape((total_blocks, 1) + (2,) * (nb - 1) + (inner, width))
    exchanges = list(reversed([bit for bit in bits if bit[0] == "coarse"]))
    assert nb >= len(exchanges) + 1
    arriving = lax.ppermute(packed, exchanges[0][0], pairs(*exchanges[0]))
    xors = [0, exchanges[0][1]]
    extended, inverse_blocks, whole, arriving = lax.optimization_barrier((extended, inverse_blocks, whole, arriving))
    packed = jnp.concatenate([packed, arriving], axis=0)
    arriving = None
    parts = [lax.slice_in_dim(whole, s * per, (s + 1) * per, axis=0) for s in range(streams)]
    split_at = (3 * margin.shape[0]) // 4
    picked = jnp.take(extended, margin[:split_at], axis=0)
    local = [jnp.einsum("jerb,jebc->jrc", picked, inverse_blocks[:split_at], preferred_element_type=jnp.float32)]
    for step in range(1, nb):
        parts = [halve(x, 1 + orders[s][step], *bits[orders[s][step]], jnp.float32) for s, x in enumerate(parts)]
        if step == 1:
            local[0], extended, parts = lax.optimization_barrier((local[0], extended, parts))
            picked = jnp.take(extended, margin[split_at:], axis=0)
            local.append(jnp.einsum("jerb,jebc->jrc", picked, inverse_blocks[split_at:], preferred_element_type=jnp.float32))
        k = step
        if arriving is not None:
            arriving, parts = lax.optimization_barrier((arriving, parts))
            packed = jnp.concatenate([packed, arriving], axis=0)
            arriving = None
        if k < len(exchanges):
            packed, parts = lax.optimization_barrier((packed, parts))
            axis, mask = exchanges[k]
            arriving = lax.ppermute(packed, axis, pairs(axis, mask))
            xors = xors + [x ^ mask for x in xors]
    assert arriving is None
    slot_of = jnp.array([xors.index(x) for x in range(len(xors))], jnp.int32)
    labels = jnp.arange(len(xors) * own_rows, dtype=jnp.int32)
    order = slot_of[(labels // own_rows) ^ lax.axis_index("coarse")] * own_rows + labels % own_rows
    inverse_all = packed[:, :, :rows, :]
    pattern_all = packed[:, :, rows, 0].astype(jnp.int32)
    mine = jnp.concatenate(parts, axis=0).reshape(total_blocks, inner, width)
    coarse_in = mine.astype(jnp.bfloat16)
    chosen = jnp.take(coarse_in, pattern_all, axis=0)
    solved = jnp.einsum(
        "nerc,necd->nrd", chosen, inverse_all, preferred_element_type=jnp.float32
    ).astype(jnp.bfloat16)
    solved = jnp.take(solved, order, axis=0)
    solved = solved.reshape((total_blocks,) + (1,) * nb + (inner, width))
    outs = [lax.slice_in_dim(solved, s * per, (s + 1) * per, axis=0) for s in range(streams)]
    for step in reversed(range(1, nb)):
        outs = [double(y, 1 + orders[s][step], *bits[orders[s][step]]) for s, y in enumerate(outs)]
        if step == nb - 1:
            local[1], outs = lax.optimization_barrier((local[1], outs))
    own = jnp.concatenate(outs, axis=0).reshape(total_blocks, rhs // 2, width)
    got = lax.ppermute(own, bits[0][0], pairs(*bits[0]))
    own_rows = jnp.take(own, interface, axis=0)
    got_rows = jnp.take(got, interface, axis=0)
    lifted = jnp.where(
        own_half == 0,
        jnp.concatenate([own_rows, got_rows], axis=2),
        jnp.concatenate([got_rows, own_rows], axis=2),
    )

    spread = jnp.einsum("jqrc,jqbc->jrb", lifted, basis, preferred_element_type=jnp.float32)
    return (jnp.concatenate(local, axis=0) + spread).astype(jnp.bfloat16)


def solution(mesh):
    in_specs = (
        P(("sub", "coarse"), None, None),
        P(("sub", "coarse"), None),
        P(("sub", "coarse"), None, None, None),
        P(("sub", "coarse"), None),
        P(("sub", "coarse"), None, None, None),
        P("coarse", None),
        P("coarse", None, None, None),
    )
    out_specs = P(("sub", "coarse"), None, None)
    return jax.shard_map(
        per_device, mesh=mesh, in_specs=in_specs, out_specs=out_specs, check_vma=False
    )
```

```python
import functools

import jax
import jax.numpy as jnp
from jax import lax
from jax.experimental import pallas as pl
from jax.experimental.pallas import tpu as pltpu
from jax.sharding import PartitionSpec as P


def restrict_kernel(links, half, residual_ref, basis_ref, out_ref, *, upper):
    j = pl.program_id(0)
    pairs_per = basis_ref.shape[1]
    rows = out_ref.shape[1]

    @pl.when(j == 0)
    def _():
        out_ref[...] = jnp.zeros_like(out_ref)

    for q in range(pairs_per):
        n = links[j * pairs_per + q]

        @pl.when(half[0] == upper)
        def _():
            out_ref[n] += jnp.dot(residual_ref[0, :rows], basis_ref[0, q], preferred_element_type=jnp.float32)

        @pl.when(half[0] != upper)
        def _():
            out_ref[n] += jnp.dot(residual_ref[0, rows:], basis_ref[0, q], preferred_element_type=jnp.float32)


def restrict(residual, basis, links, total_blocks, half, upper):
    count, rhs, size = residual.shape
    width = basis.shape[-1]
    rows = rhs // 2
    return pl.pallas_call(
        functools.partial(restrict_kernel, upper=upper),
        out_shape=jax.ShapeDtypeStruct((total_blocks, rows, width), jnp.float32),
        grid_spec=pltpu.PrefetchScalarGridSpec(
            num_scalar_prefetch=2,
            grid=(count,),
            in_specs=[
                pl.BlockSpec((1, rhs, size), lambda j, links, half: (j, 0, 0)),
                pl.BlockSpec((1, basis.shape[1], size, width), lambda j, links, half: (j, 0, 0, 0)),
            ],
            out_specs=pl.BlockSpec((total_blocks, rows, width), lambda j, links, half: (0, 0, 0)),
        ),
        compiler_params=pltpu.CompilerParams(dimension_semantics=("arbitrary",)),
        cost_estimate=pl.CostEstimate(
            flops=count * basis.shape[1] * rhs * size * width,
            bytes_accessed=residual.size * 2 + basis.size * 2 + total_blocks * rows * width * 4,
            transcendentals=0,
        ),
    )(links, half, residual, basis)


def with_halo(cells, sides, width):
    for axis, dim in sides:
        count = lax.axis_size(axis)
        ends = count - 1
        head = lax.slice_in_dim(cells, 0, width, axis=dim)
        tail = lax.slice_in_dim(cells, cells.shape[dim] - width, cells.shape[dim], axis=dim)
        cells = jnp.concatenate(
            [
                lax.ppermute(tail, axis, [(i, (i + 1) % count) for i in range(ends)]),
                cells,
                lax.ppermute(head, axis, [((i + 1) % count, i) for i in range(ends)]),
            ],
            axis=dim,
        )
    return cells


def device_bits():
    bits = []
    for axis in ("coarse", "sub"):
        size = lax.axis_size(axis)
        mask = 1
        while mask < size:
            bits.append((axis, mask))
            mask *= 2
        assert mask == size
    return bits


def bit_of(axis, mask):
    return (lax.axis_index(axis) // mask) % 2


def pairs(axis, mask):
    return [(i, i ^ mask) for i in range(lax.axis_size(axis))]


def halve(x, dim, axis, mask, wire):
    v = bit_of(axis, mask)
    keep = lax.dynamic_index_in_dim(x, v, axis=dim, keepdims=True)
    send = lax.dynamic_index_in_dim(x, 1 - v, axis=dim, keepdims=True)
    return keep + lax.ppermute(send.astype(wire), axis, pairs(axis, mask)).astype(x.dtype)


def double(y, dim, axis, mask):
    v = bit_of(axis, mask)
    recv = lax.ppermute(y, axis, pairs(axis, mask))
    return jnp.where(v == 0, jnp.concatenate([y, recv], axis=dim), jnp.concatenate([recv, y], axis=dim))


def stream_orders(nbits, streams):
    rest = list(range(1, nbits))
    orders = []
    for s in range(streams):
        k = (s * len(rest)) // streams
        orders.append([0] + rest[k:] + rest[:k])
    return orders


def per_device(residual, margin, inverse_blocks, interface, basis, coarse_pattern, coarse_inverse):
    rows, cols = coarse_inverse.shape[-2:]
    tags = jnp.broadcast_to(coarse_pattern.astype(jnp.bfloat16)[:, :, None, None], coarse_pattern.shape + (8, cols))
    packed = jnp.concatenate([coarse_inverse, tags], axis=2)
    own_rows = coarse_inverse.shape[0]
    extended = with_halo(residual, ((("sub", "coarse"), 0),), 1)
    rhs = residual.shape[1]
    width = basis.shape[-1]
    total_blocks = own_rows * lax.axis_size("coarse")
    bits = device_bits()
    own_half = bit_of(*bits[0])
    links = interface.reshape(-1)
    half = own_half.reshape(1).astype(jnp.int32)
    send = restrict(residual, basis, links, total_blocks, half, 1)

    nb = len(bits)
    inner = rhs >> nb
    assert inner << nb == rhs
    streams = 3 if total_blocks % 3 == 0 else 1
    per = total_blocks // streams
    orders = stream_orders(nb, streams)
    got = lax.ppermute(send, bits[0][0], pairs(*bits[0]))
    whole = restrict(residual, basis, links, total_blocks, half, 0) + got
    whole = whole.reshape((total_blocks, 1) + (2,) * (nb - 1) + (inner, width))
    exchanges = list(reversed([bit for bit in bits if bit[0] == "coarse"]))
    assert nb >= len(exchanges) + 1
    arriving = lax.ppermute(packed, exchanges[0][0], pairs(*exchanges[0]))
    xors = [0, exchanges[0][1]]
    extended, inverse_blocks, whole, arriving = lax.optimization_barrier((extended, inverse_blocks, whole, arriving))
    packed = jnp.concatenate([packed, arriving], axis=0)
    arriving = None
    parts = [lax.slice_in_dim(whole, s * per, (s + 1) * per, axis=0) for s in range(streams)]
    split_at = (3 * margin.shape[0]) // 4
    picked = jnp.take(extended, margin[:split_at], axis=0)
    local = [jnp.einsum("jerb,jebc->jrc", picked, inverse_blocks[:split_at], preferred_element_type=jnp.float32)]
    for step in range(1, nb):
        parts = [halve(x, 1 + orders[s][step], *bits[orders[s][step]], jnp.float32) for s, x in enumerate(parts)]
        if step == 1:
            local[0], extended, parts = lax.optimization_barrier((local[0], extended, parts))
            picked = jnp.take(extended, margin[split_at:], axis=0)
            local.append(jnp.einsum("jerb,jebc->jrc", picked, inverse_blocks[split_at:], preferred_element_type=jnp.float32))
        if step == 3:
            local[1], parts = lax.optimization_barrier((local[1], parts))
        k = step
        if arriving is not None:
            arriving, parts = lax.optimization_barrier((arriving, parts))
            packed = jnp.concatenate([packed, arriving], axis=0)
            arriving = None
        if k < len(exchanges):
            packed, parts = lax.optimization_barrier((packed, parts))
            axis, mask = exchanges[k]
            arriving = lax.ppermute(packed, axis, pairs(axis, mask))
            xors = xors + [x ^ mask for x in xors]
    assert arriving is None
    slot_of = jnp.array([xors.index(x) for x in range(len(xors))], jnp.int32)
    labels = jnp.arange(len(xors) * own_rows, dtype=jnp.int32)
    order = slot_of[(labels // own_rows) ^ lax.axis_index("coarse")] * own_rows + labels % own_rows
    inverse_all = packed[:, :, :rows, :]
    pattern_all = packed[:, :, rows, 0].astype(jnp.int32)
    mine = jnp.concatenate(parts, axis=0).reshape(total_blocks, inner, width)
    coarse_in = mine.astype(jnp.bfloat16)
    chosen = jnp.take(coarse_in, pattern_all, axis=0)
    solved = jnp.einsum(
        "nerc,necd->nrd", chosen, inverse_all, preferred_element_type=jnp.float32
    ).astype(jnp.bfloat16)
    solved = jnp.take(solved, order, axis=0)
    solved = solved.reshape((total_blocks,) + (1,) * nb + (inner, width))
    outs = [lax.slice_in_dim(solved, s * per, (s + 1) * per, axis=0) for s in range(streams)]
    for step in reversed(range(1, nb)):
        outs = [double(y, 1 + orders[s][step], *bits[orders[s][step]]) for s, y in enumerate(outs)]
    own = jnp.concatenate(outs, axis=0).reshape(total_blocks, rhs // 2, width)
    got = lax.ppermute(own, bits[0][0], pairs(*bits[0]))
    own_rows = jnp.take(own, interface, axis=0)
    got_rows = jnp.take(got, interface, axis=0)
    lifted = jnp.where(
        own_half == 0,
        jnp.concatenate([own_rows, got_rows], axis=2),
        jnp.concatenate([got_rows, own_rows], axis=2),
    )

    spread = jnp.einsum("jqrc,jqbc->jrb", lifted, basis, preferred_element_type=jnp.float32)
    return (jnp.concatenate(local, axis=0) + spread).astype(jnp.bfloat16)


def solution(mesh):
    in_specs = (
        P(("sub", "coarse"), None, None),
        P(("sub", "coarse"), None),
        P(("sub", "coarse"), None, None, None),
        P(("sub", "coarse"), None),
        P(("sub", "coarse"), None, None, None),
        P("coarse", None),
        P("coarse", None, None, None),
    )
    out_specs = P(("sub", "coarse"), None, None)
    return jax.shard_map(
        per_device, mesh=mesh, in_specs=in_specs, out_specs=out_specs, check_vma=False
    )
```

```python
import functools

import jax
import jax.numpy as jnp
from jax import lax
from jax.experimental import pallas as pl
from jax.experimental.pallas import tpu as pltpu
from jax.sharding import PartitionSpec as P


def restrict_kernel(links, half, residual_ref, basis_ref, out_ref, *, upper):
    j = pl.program_id(0)
    pairs_per = basis_ref.shape[1]
    rows = out_ref.shape[1]

    @pl.when(j == 0)
    def _():
        out_ref[...] = jnp.zeros_like(out_ref)

    for q in range(pairs_per):
        n = links[q * pl.num_programs(0) + j]

        @pl.when(half[0] == upper)
        def _():
            out_ref[n] += jnp.dot(residual_ref[0, :rows], basis_ref[0, q], preferred_element_type=jnp.float32)

        @pl.when(half[0] != upper)
        def _():
            out_ref[n] += jnp.dot(residual_ref[0, rows:], basis_ref[0, q], preferred_element_type=jnp.float32)


def restrict(residual, basis, links, total_blocks, half, upper):
    count, rhs, size = residual.shape
    width = basis.shape[-1]
    rows = rhs // 2
    return pl.pallas_call(
        functools.partial(restrict_kernel, upper=upper),
        out_shape=jax.ShapeDtypeStruct((total_blocks, rows, width), jnp.float32),
        grid_spec=pltpu.PrefetchScalarGridSpec(
            num_scalar_prefetch=2,
            grid=(count,),
            in_specs=[
                pl.BlockSpec((1, rhs, size), lambda j, links, half: (j, 0, 0)),
                pl.BlockSpec((1, basis.shape[1], size, width), lambda j, links, half: (j, 0, 0, 0)),
            ],
            out_specs=pl.BlockSpec((total_blocks, rows, width), lambda j, links, half: (0, 0, 0)),
        ),
        compiler_params=pltpu.CompilerParams(dimension_semantics=("arbitrary",)),
        cost_estimate=pl.CostEstimate(
            flops=count * basis.shape[1] * rhs * size * width,
            bytes_accessed=residual.size * 2 + basis.size * 2 + total_blocks * rows * width * 4,
            transcendentals=0,
        ),
    )(links, half, residual, basis)


def with_halo(cells, sides, width):
    for axis, dim in sides:
        count = lax.axis_size(axis)
        ends = count - 1
        head = lax.slice_in_dim(cells, 0, width, axis=dim)
        tail = lax.slice_in_dim(cells, cells.shape[dim] - width, cells.shape[dim], axis=dim)
        cells = jnp.concatenate(
            [
                lax.ppermute(tail, axis, [(i, (i + 1) % count) for i in range(ends)]),
                cells,
                lax.ppermute(head, axis, [((i + 1) % count, i) for i in range(ends)]),
            ],
            axis=dim,
        )
    return cells


def device_bits():
    bits = []
    for axis in ("coarse", "sub"):
        size = lax.axis_size(axis)
        mask = 1
        while mask < size:
            bits.append((axis, mask))
            mask *= 2
        assert mask == size
    return bits


def bit_of(axis, mask):
    return (lax.axis_index(axis) // mask) % 2


def pairs(axis, mask):
    return [(i, i ^ mask) for i in range(lax.axis_size(axis))]


def halve(x, dim, axis, mask, wire):
    v = bit_of(axis, mask)
    keep = lax.dynamic_index_in_dim(x, v, axis=dim, keepdims=True)
    send = lax.dynamic_index_in_dim(x, 1 - v, axis=dim, keepdims=True)
    return keep + lax.ppermute(send.astype(wire), axis, pairs(axis, mask)).astype(x.dtype)


def double(y, dim, axis, mask):
    v = bit_of(axis, mask)
    recv = lax.ppermute(y, axis, pairs(axis, mask))
    return jnp.where(v == 0, jnp.concatenate([y, recv], axis=dim), jnp.concatenate([recv, y], axis=dim))


def stream_orders(nbits, streams):
    rest = list(range(1, nbits))
    orders = []
    for s in range(streams):
        k = (s * len(rest)) // streams
        orders.append([0] + rest[k:] + rest[:k])
    return orders


def per_device(residual, margin, inverse_blocks, interface, basis, coarse_pattern, coarse_inverse):
    rows, cols = coarse_inverse.shape[-2:]
    tags = jnp.broadcast_to(coarse_pattern.astype(jnp.bfloat16)[:, :, None, None], coarse_pattern.shape + (8, cols))
    packed = jnp.concatenate([coarse_inverse, tags], axis=2)
    own_rows = coarse_inverse.shape[0]
    extended = with_halo(residual, ((("sub", "coarse"), 0),), 1)
    rhs = residual.shape[1]
    width = basis.shape[-1]
    total_blocks = own_rows * lax.axis_size("coarse")
    bits = device_bits()
    own_half = bit_of(*bits[0])
    links = jnp.concatenate([interface[:, q] for q in range(interface.shape[1])])
    half = own_half.reshape(1).astype(jnp.int32)
    send = restrict(residual, basis, links, total_blocks, half, 1)

    nb = len(bits)
    inner = rhs >> nb
    assert inner << nb == rhs
    streams = 3 if total_blocks % 3 == 0 else 1
    per = total_blocks // streams
    orders = stream_orders(nb, streams)
    got = lax.ppermute(send, bits[0][0], pairs(*bits[0]))
    whole = restrict(residual, basis, links, total_blocks, half, 0) + got
    whole = whole.reshape((total_blocks, 1) + (2,) * (nb - 1) + (inner, width))
    exchanges = list(reversed([bit for bit in bits if bit[0] == "coarse"]))
    assert nb >= len(exchanges) + 1
    arriving = lax.ppermute(packed, exchanges[0][0], pairs(*exchanges[0]))
    xors = [0, exchanges[0][1]]
    extended, inverse_blocks, whole, arriving = lax.optimization_barrier((extended, inverse_blocks, whole, arriving))
    packed = jnp.concatenate([packed, arriving], axis=0)
    arriving = None
    parts = [lax.slice_in_dim(whole, s * per, (s + 1) * per, axis=0) for s in range(streams)]
    split_at = (3 * margin.shape[0]) // 4
    picked = jnp.take(extended, margin[:split_at], axis=0)
    local = [jnp.einsum("jerb,jebc->jrc", picked, inverse_blocks[:split_at], preferred_element_type=jnp.float32)]
    for step in range(1, nb):
        parts = [halve(x, 1 + orders[s][step], *bits[orders[s][step]], jnp.float32) for s, x in enumerate(parts)]
        if step == 1:
            local[0], extended, parts = lax.optimization_barrier((local[0], extended, parts))
            picked = jnp.take(extended, margin[split_at:], axis=0)
            local.append(jnp.einsum("jerb,jebc->jrc", picked, inverse_blocks[split_at:], preferred_element_type=jnp.float32))
        if step == 2:
            local[1], parts = lax.optimization_barrier((local[1], parts))
        k = step
        if arriving is not None:
            arriving, parts = lax.optimization_barrier((arriving, parts))
            packed = jnp.concatenate([packed, arriving], axis=0)
            arriving = None
        if k < len(exchanges):
            packed, parts = lax.optimization_barrier((packed, parts))
            axis, mask = exchanges[k]
            arriving = lax.ppermute(packed, axis, pairs(axis, mask))
            xors = xors + [x ^ mask for x in xors]
    assert arriving is None
    slot_of = jnp.array([xors.index(x) for x in range(len(xors))], jnp.int32)
    labels = jnp.arange(len(xors) * own_rows, dtype=jnp.int32)
    order = slot_of[(labels // own_rows) ^ lax.axis_index("coarse")] * own_rows + labels % own_rows
    inverse_all = packed[:, :, :rows, :]
    pattern_all = packed[:, :, rows, 0].astype(jnp.int32)
    mine = jnp.concatenate(parts, axis=0).reshape(total_blocks, inner, width)
    coarse_in = mine.astype(jnp.bfloat16)
    chosen = jnp.take(coarse_in, pattern_all, axis=0)
    solved = jnp.einsum(
        "nerc,necd->nrd", chosen, inverse_all, preferred_element_type=jnp.float32
    ).astype(jnp.bfloat16)
    solved = jnp.take(solved, order, axis=0)
    solved = solved.reshape((total_blocks,) + (1,) * nb + (inner, width))
    outs = [lax.slice_in_dim(solved, s * per, (s + 1) * per, axis=0) for s in range(streams)]
    for step in reversed(range(1, nb)):
        outs = [double(y, 1 + orders[s][step], *bits[orders[s][step]]) for s, y in enumerate(outs)]
    own = jnp.concatenate(outs, axis=0).reshape(total_blocks, rhs // 2, width)
    got = lax.ppermute(own, bits[0][0], pairs(*bits[0]))
    own_rows = jnp.take(own, interface, axis=0)
    got_rows = jnp.take(got, interface, axis=0)
    lifted = jnp.where(
        own_half == 0,
        jnp.concatenate([own_rows, got_rows], axis=2),
        jnp.concatenate([got_rows, own_rows], axis=2),
    )

    spread = jnp.einsum("jqrc,jqbc->jrb", lifted, basis, preferred_element_type=jnp.float32)
    return (jnp.concatenate(local, axis=0) + spread).astype(jnp.bfloat16)


def solution(mesh):
    in_specs = (
        P(("sub", "coarse"), None, None),
        P(("sub", "coarse"), None),
        P(("sub", "coarse"), None, None, None),
        P(("sub", "coarse"), None),
        P(("sub", "coarse"), None, None, None),
        P("coarse", None),
        P("coarse", None, None, None),
    )
    out_specs = P(("sub", "coarse"), None, None)
    return jax.shard_map(
        per_device, mesh=mesh, in_specs=in_specs, out_specs=out_specs, check_vma=False
    )
```
